256 devices in a mesh: ctx: 32 (over x, z_lo, y), head: 8 (over z_hi, core).
Axes of the slice: x: 4, y: 4, z: 8 (z_hi: 4, z_lo: 2; z = z_hi * 2 + z_lo), core: 2. Of those that a mesh axis runs over, the one named last changes fastest.
Arguments:
- tokens: bfloat16 [8192, 4096], P('ctx', 'head'), may hold values from -6 to 6
- cotangent: bfloat16 [8192, 4096], P('ctx', 'head'), may hold values from -0.1796875 to 0.1796875
- expert_ids: int32 [8192, 2], P('ctx'), may hold values from 0 to 31, all different within a row; in each aligned block of 256 rows (0 to 255, 256 to 511, ...) at most 24 rows name the same one
- w_router: bfloat16 [4096, 32], P('head'), may hold values from -0.09375 to 0.09375
- w_gate: bfloat16 [32, 1408, 4096], P('ctx', None, 'head'), may hold values from -0.09375 to 0.09375
- w_up: bfloat16 [32, 1408, 4096], P('ctx', None, 'head'), may hold values from -0.09375 to 0.09375
- w_down: bfloat16 [32, 1408, 4096], P('ctx', None, 'head'), may hold values from -0.15625 to 0.15625
Outputs:
- mixed: bfloat16 [8192, 4096], P('ctx', 'head')
- grad_tokens: bfloat16 [8192, 4096], P('ctx', 'head')
- grad_router: float32 [4096, 32], P('head')
- grad_gate: bfloat16 [32, 1408, 4096], P('ctx', None, 'head')
- grad_up: bfloat16 [32, 1408, 4096], P('ctx', None, 'head')
- grad_down: bfloat16 [32, 1408, 4096], P('ctx', None, 'head')
The draws below stay inside these ranges and needn't reach their ends.
Inputs may be any that keep to these rules, and one draw needn't show every extreme that they name: `expert_ids`: each row names 2 different experts. Within the rows of one device (aligned blocks of 256 rows) no expert is named by more than 24 rows, a bound that some block reaches.
All inputs are finite; a program needn't handle non-finite values.
Results may differ from the reference program's by a relative error of at most 0.023.
Values may be sent and summed in bfloat16 or wider, within the bound.
No kernel may reach another device: no remote copies, remote signals or barrier semaphores. Data moves between devices by JAX's collectives and lax.ppermute only.
A program may use at most 64 MiB of HBM per device.

```python
import math
import jax
import jax.numpy as jnp
import numpy as np
from jax import lax

D = 4096
FF = 1408
TOPK = 2
TOK_DEV = 256
EXPERTS = 32
TOKENS = 8192
CAP = 24
N_CTX = 32
N_HEAD = 8


def levels(key, dims, pieces, low, largest):
    def one(position, blocks):
        heights = jax.random.uniform(jax.random.fold_in(jax.random.fold_in(key, 6), position), (blocks,), jnp.float32, low / len(pieces), largest / len(pieces))
        return jnp.repeat(jnp.exp(heights), dims[position] // blocks).reshape((-1,) + (1,) * (len(dims) - position - 1))

    factor_of = one(*pieces[0])
    for cut in pieces[1:]:
        factor_of = factor_of * one(*cut)
    return factor_of


def deal_out(stream_key, own, number, rows, number_of, top, limit, lean):
    ranking = jax.random.permutation(stream_key, number_of)
    packed, common = shares(number_of, rows * top, limit, lean, True), shares(number_of, rows * top, limit, lean, False)
    places = jnp.arange(number_of)

    def named(lengths, offset_by):
        used = int((lengths > 0).sum())
        fixed = max(1, used // 4)
        moved = fixed + (places - fixed + offset_by * (used - fixed)) % max(1, number_of - fixed)
        return jnp.zeros((number_of,), jnp.int32).at[ranking[jnp.where(places < fixed, places, moved)]].set(jnp.asarray(lengths, jnp.int32))

    lengths = jnp.where(number % 4 == 0, named(packed, number // 4), named(common, number - number // 4 - 1))
    mixed = jax.random.permutation(jax.random.fold_in(own, 3), number_of)
    giver, sink = mixed[0:number_of // 2 * 2:2], mixed[1:number_of // 2 * 2:2]
    room = jnp.minimum(lengths[giver] - 1, limit - lengths[sink]) // 2
    room = jnp.where((giver == ranking[0]) | (sink == ranking[0]) | (lengths[sink] == 0), 0, jnp.maximum(room, 0))
    moved = jax.random.randint(jax.random.fold_in(own, 4), (number_of // 2,), 0, 1 << 20) % (room + 1)
    lengths = lengths.at[giver].add(-moved).at[sink].add(moved)
    labels = jnp.searchsorted(jnp.cumsum(lengths), jnp.arange(rows * top), side="right").astype(jnp.int32)
    table = labels.reshape(top, rows).T
    table = table[jax.random.permutation(jax.random.fold_in(own, 1), rows)]
    offset_by = jax.random.randint(jax.random.fold_in(own, 2), (rows, 1), 0, top)
    return jnp.take_along_axis(table, (jnp.arange(top)[None, :] + offset_by) % top, axis=1)


def shares(amount, total, reach, slope, full):
    weights = [(1 << 20) // math.isqrt(standing ** slope) + 1 for standing in range(1, amount + 1)]
    largest = reach if full else min(reach, max(-(-total // amount), total * weights[0] // sum(weights)))
    least = 1 if total - largest >= amount - 1 else 0
    counts, rest = [largest] + [least] * (amount - 1), total - largest - least * (amount - 1)
    while rest > 0:
        movable = [i for i in range(1, amount) if counts[i] < largest] or [i for i in range(1, amount) if counts[i] < reach]
        whole, remaining = sum([weights[i] for i in movable]), rest
        for i in movable:
            more = min(reach - counts[i], max(1, remaining * weights[i] // whole), rest)
            counts[i] = counts[i] + more
            rest = rest - more
    return np.array(counts)


def normal_values(stream_key, extent, spread, most, pieces=(), kind=jnp.bfloat16):
    values = spread * jax.random.normal(stream_key, extent, jnp.float32)
    if pieces:
        values = values * levels(stream_key, extent, pieces, -0.22, 0.18)
    return jnp.clip(values, -most, most).astype(kind)


def setup_inputs(seed: int = 0) -> dict:
    key_of = jax.random.split(jax.random.key(seed), 8)
    tokens = normal_values(key_of[0], (TOKENS, D), 1.0, 6.0, ((0, 32), (1, 8)))
    cotangent = normal_values(key_of[1], (TOKENS, D), 0.03, 0.1796875, ((0, 32), (1, 8)))
    expert_ids_keys = jax.random.split(jax.random.fold_in(key_of[2], 1), TOKENS // TOK_DEV)
    expert_ids_turns = jax.random.permutation(jax.random.fold_in(key_of[2], 3), TOKENS // TOK_DEV)
    expert_ids = jax.vmap(lambda own, number: deal_out(jax.random.fold_in(key_of[2], 2), own, number, TOK_DEV, EXPERTS, TOPK, CAP, 2))(expert_ids_keys, expert_ids_turns).reshape((TOKENS, TOPK))
    w_router = normal_values(key_of[3], (D, EXPERTS), D ** -0.5, 0.09375, ((0, 8),))
    w_gate = normal_values(key_of[4], (EXPERTS, FF, D), D ** -0.5, 0.09375, ((0, 32), (2, 8)))
    w_up = normal_values(key_of[5], (EXPERTS, FF, D), D ** -0.5, 0.09375, ((0, 32), (2, 8)))
    w_down = normal_values(key_of[6], (EXPERTS, FF, D), FF ** -0.5, 0.15625, ((0, 32), (2, 8)))
    return dict(tokens=tokens, cotangent=cotangent, expert_ids=expert_ids, w_router=w_router, w_gate=w_gate, w_up=w_up, w_down=w_down)


def split_in(rows, weight):
    group = D // N_HEAD
    count = rows.shape[0]
    part_sums = jnp.einsum("rgd,fgd->grf", rows.reshape(count, N_HEAD, group).astype(jnp.float32), weight.reshape(FF, N_HEAD, group).astype(jnp.float32)).astype(jnp.bfloat16)
    part_sums = lax.optimization_barrier(part_sums)
    return jnp.sum(part_sums.astype(jnp.float32), axis=0)


def reference(tokens, cotangent, expert_ids, w_router, w_gate, w_up, w_down):
    logits = jnp.dot(tokens, w_router, preferred_element_type=jnp.float32)
    onehot = (expert_ids[:, :, None] == jnp.arange(EXPERTS, dtype=jnp.int32)[None, None, :]).astype(jnp.float32)
    chosen = jnp.sum(logits[:, None, :] * onehot, axis=2)
    prob_pairs = jnp.stack([jax.nn.sigmoid(chosen[:, 0] - chosen[:, 1]), jax.nn.sigmoid(chosen[:, 1] - chosen[:, 0])], axis=1)
    block_ids = expert_ids.reshape(N_CTX, TOK_DEV * TOPK)
    id_hits = (block_ids[:, :, None] == jnp.arange(EXPERTS, dtype=jnp.int32)[None, None, :]).astype(jnp.int32)
    places = jnp.sum((jnp.cumsum(id_hits, axis=1) - 1) * id_hits, axis=2).astype(jnp.int32)
    slot_rows = N_CTX * CAP
    sources = jnp.arange(N_CTX, dtype=jnp.int32)[:, None]
    slot_index = (block_ids * slot_rows + sources * CAP + places).reshape(-1).astype(jnp.int32)
    slot_table = jnp.zeros((EXPERTS * slot_rows,), jnp.int32).at[slot_index].set(jnp.arange(TOKENS * TOPK, dtype=jnp.int32) + 1)
    slot_table = slot_table.reshape(EXPERTS, slot_rows)
    prob_flat = prob_pairs.reshape(-1)

    def one_expert(expert_args):
        entries, gate_w, up_w, down_w = expert_args
        occupied = entries > 0
        source = jnp.maximum(entries - 1, 0)
        row_index = source // TOPK
        x_rows = jnp.where(occupied[:, None], tokens[row_index], jnp.zeros((), jnp.bfloat16)).astype(jnp.bfloat16)
        cot_rows = jnp.where(occupied[:, None], cotangent[row_index], jnp.zeros((), jnp.bfloat16)).astype(jnp.bfloat16)
        prob_rows = jnp.where(occupied, prob_flat[source], jnp.float32(0.0))
        gate_pre = split_in(x_rows, gate_w)
        up_pre = split_in(x_rows, up_w)
        back_proj = split_in(cot_rows, down_w)
        sigma = jax.nn.sigmoid(gate_pre)
        active = gate_pre * sigma
        hidden = (active * up_pre).astype(jnp.bfloat16)
        expert_out = jnp.dot(hidden, down_w, preferred_element_type=jnp.float32).astype(jnp.bfloat16)
        hidden_grad = prob_rows[:, None] * back_proj
        gate_grad = (hidden_grad * up_pre * sigma * (1.0 + gate_pre * (1.0 - sigma))).astype(jnp.bfloat16)
        up_grad = (hidden_grad * active).astype(jnp.bfloat16)
        expert_dx = (jnp.dot(gate_grad, gate_w, preferred_element_type=jnp.float32) + jnp.dot(up_grad, up_w, preferred_element_type=jnp.float32)).astype(jnp.bfloat16)
        hidden_kept = lax.optimization_barrier(hidden)
        scaled = (prob_rows[:, None] * hidden_kept.astype(jnp.float32)).astype(jnp.bfloat16)
        grad_down = jnp.dot(scaled.T, cot_rows, preferred_element_type=jnp.float32).astype(jnp.bfloat16)
        grad_gate = jnp.dot(gate_grad.T, x_rows, preferred_element_type=jnp.float32).astype(jnp.bfloat16)
        grad_up = jnp.dot(up_grad.T, x_rows, preferred_element_type=jnp.float32).astype(jnp.bfloat16)
        return expert_out, expert_dx, grad_gate, grad_up, grad_down

    expert_out, expert_dx, grad_gate, grad_up, grad_down = lax.map(one_expert, (slot_table, w_gate, w_up, w_down))
    out_pairs = expert_out.reshape(EXPERTS * slot_rows, D)[slot_index].reshape(TOKENS, TOPK, D)
    dx_pairs = expert_dx.reshape(EXPERTS * slot_rows, D)[slot_index].reshape(TOKENS, TOPK, D)
    mixed = jnp.sum(prob_pairs[:, :, None] * out_pairs.astype(jnp.float32), axis=1).astype(jnp.bfloat16)
    score_grad = jnp.sum(cotangent.astype(jnp.float32)[:, None, :] * out_pairs.astype(jnp.float32), axis=2)
    logit_lead = prob_pairs[:, 0] * prob_pairs[:, 1] * (score_grad[:, 0] - score_grad[:, 1])
    logit_grad = jnp.stack([logit_lead, -logit_lead], axis=1)
    dense_grad = jnp.sum(logit_grad[:, :, None] * onehot, axis=1)
    router_term = jnp.dot(dense_grad, w_router.astype(jnp.float32).T, precision=lax.Precision.HIGHEST)
    grad_tokens = (dx_pairs[:, 0].astype(jnp.float32) + dx_pairs[:, 1].astype(jnp.float32) + router_term).astype(jnp.bfloat16)
    grad_router = jnp.dot(tokens.astype(jnp.float32).T, dense_grad, precision=lax.Precision.HIGHEST)
    return mixed, grad_tokens, grad_router, grad_gate, grad_up, grad_down
```

```python
import jax
import jax.numpy as jnp
from jax import lax
from jax.sharding import PartitionSpec as P


def contract_rows(left, right):
    return lax.dot_general(
        left, right, (((0,), (0,)), ((), ())), preferred_element_type=jnp.float32
    )


def contract_last(left, right):
    return lax.dot_general(
        left, right, (((1,), (1,)), ((), ())), preferred_element_type=jnp.float32
    )


def activations(gate_pre, up_pre, back_proj, prob_rows):
    sigma = jax.nn.sigmoid(gate_pre)
    active = gate_pre * sigma
    hidden = (active * up_pre).astype(jnp.bfloat16)
    hidden_grad = prob_rows[:, None] * back_proj
    gate_grad = (hidden_grad * up_pre * sigma * (1.0 + gate_pre * (1.0 - sigma))).astype(
        jnp.bfloat16
    )
    up_grad = (hidden_grad * active).astype(jnp.bfloat16)
    return (hidden, gate_grad, up_grad)


def head_sum(part):
    count = lax.axis_size("head")
    spread = jnp.broadcast_to(part[None], (count,) + part.shape)
    gathered = lax.all_to_all(spread, "head", split_axis=0, concat_axis=0, tiled=True)
    return jnp.sum(gathered, axis=0)


def ctx_sum(part):
    count = lax.axis_size("ctx")
    rows = part.shape[0]
    pieces = part.reshape(count, rows // count, part.shape[1])
    mine = jnp.sum(lax.all_to_all(pieces, "ctx", split_axis=0, concat_axis=0, tiled=True), axis=0)
    spread = jnp.broadcast_to(mine[None], pieces.shape)
    return lax.all_to_all(spread, "ctx", split_axis=0, concat_axis=0, tiled=True).reshape(part.shape)


def local(tokens, cotangent, expert_ids, w_router, w_gate, w_up, w_down):
    ctx_count = lax.axis_size("ctx")
    tok_rows = tokens.shape[0]
    shard_width = tokens.shape[1]
    pick_count = expert_ids.shape[1]
    experts = w_router.shape[1]
    capacity = 3 * tok_rows * pick_count // (2 * experts)
    partial_logits = jnp.dot(tokens, w_router, preferred_element_type=jnp.float32)
    onehot = (expert_ids[:, :, None] == jnp.arange(experts, dtype=jnp.int32)[None, None, :]).astype(
        jnp.float32
    )
    chosen = head_sum(jnp.sum(partial_logits[:, None, :] * onehot, axis=2))
    prob_pairs = jnp.stack(
        [jax.nn.sigmoid(chosen[:, 0] - chosen[:, 1]), jax.nn.sigmoid(chosen[:, 1] - chosen[:, 0])],
        axis=1,
    )
    flat_ids = expert_ids.reshape(-1)
    id_hits = (flat_ids[:, None] == jnp.arange(experts, dtype=jnp.int32)[None, :]).astype(jnp.int32)
    places = jnp.sum((jnp.cumsum(id_hits, axis=0) - 1) * id_hits, axis=1)
    slot_index = flat_ids * capacity + places
    slot_table = (
        jnp.zeros((experts * capacity,), jnp.int32)
        .at[slot_index]
        .set(jnp.arange(tok_rows * pick_count, dtype=jnp.int32) + 1)
    )
    occupied = slot_table > 0
    source = jnp.maximum(slot_table - 1, 0)
    row_index = source // pick_count
    prob_send = jnp.where(occupied, prob_pairs.reshape(-1)[source], jnp.float32(0.0)).reshape(
        experts, capacity
    )

    def pack_rows(values):
        picked = jnp.where(occupied[:, None], values[row_index], jnp.zeros((), values.dtype))
        return picked.reshape(experts, capacity, values.shape[1])

    recv_x, recv_g, recv_p = (
        lax.all_to_all(pack_rows(tokens), "ctx", split_axis=0, concat_axis=0, tiled=True),
        lax.all_to_all(pack_rows(cotangent), "ctx", split_axis=0, concat_axis=0, tiled=True),
        lax.all_to_all(
            prob_send.astype(jnp.bfloat16), "ctx", split_axis=0, concat_axis=0, tiled=True
        ).astype(prob_send.dtype),
    )
    slot_count = recv_x.shape[0] * recv_x.shape[1]
    x_rows = recv_x.reshape(slot_count, shard_width)
    cot_rows = recv_g.reshape(slot_count, shard_width)
    prob_rows = recv_p.reshape(slot_count)
    gate_w = w_gate[0]
    up_w = w_up[0]
    down_w = w_down[0]
    gate_part = contract_last(x_rows, gate_w)
    up_part = contract_last(x_rows, up_w)
    back_part = contract_last(cot_rows, down_w)
    gate_pre, up_pre, back_proj = (
        lax.psum(gate_part.astype(jnp.bfloat16), "head").astype(jnp.float32),
        lax.psum(up_part.astype(jnp.bfloat16), "head").astype(jnp.float32),
        lax.psum(back_part.astype(jnp.bfloat16), "head").astype(jnp.float32),
    )
    hidden, gate_grad, up_grad = activations(gate_pre, up_pre, back_proj, prob_rows)
    out_rows = jnp.dot(hidden, down_w, preferred_element_type=jnp.float32).astype(jnp.bfloat16)
    dx_rows = (
        jnp.dot(gate_grad, gate_w, preferred_element_type=jnp.float32)
        + jnp.dot(up_grad, up_w, preferred_element_type=jnp.float32)
    ).astype(jnp.bfloat16)
    hidden_kept = lax.optimization_barrier(hidden)
    scaled = (prob_rows[:, None] * hidden_kept.astype(jnp.float32)).astype(jnp.bfloat16)
    grad_down = contract_rows(scaled, cot_rows).astype(jnp.bfloat16)[None]
    grad_gate = contract_rows(gate_grad, x_rows).astype(jnp.bfloat16)[None]
    grad_up = contract_rows(up_grad, x_rows).astype(jnp.bfloat16)[None]
    back_out, back_dx = (
        lax.all_to_all(
            out_rows.reshape(ctx_count, capacity, shard_width),
            "ctx",
            split_axis=0,
            concat_axis=0,
            tiled=True,
        ),
        lax.all_to_all(
            dx_rows.reshape(ctx_count, capacity, shard_width),
            "ctx",
            split_axis=0,
            concat_axis=0,
            tiled=True,
        ),
    )
    out_pairs = back_out.reshape(experts * capacity, shard_width)[slot_index].reshape(
        tok_rows, pick_count, shard_width
    )
    dx_pairs = back_dx.reshape(experts * capacity, shard_width)[slot_index].reshape(
        tok_rows, pick_count, shard_width
    )
    mixed = jnp.sum(prob_pairs[:, :, None] * out_pairs.astype(jnp.float32), axis=1).astype(
        jnp.bfloat16
    )
    score_part = jnp.sum(
        cotangent.astype(jnp.float32)[:, None, :] * out_pairs.astype(jnp.float32), axis=2
    )
    score_grad = head_sum(score_part)
    logit_lead = prob_pairs[:, 0] * prob_pairs[:, 1] * (score_grad[:, 0] - score_grad[:, 1])
    logit_grad = jnp.stack([logit_lead, -logit_lead], axis=1)
    dense_grad = jnp.sum(logit_grad[:, :, None] * onehot, axis=1)
    router_term = jnp.dot(
        dense_grad, w_router.astype(jnp.float32).T, precision=lax.Precision.HIGHEST
    )
    grad_tokens = (
        dx_pairs[:, 0].astype(jnp.float32) + dx_pairs[:, 1].astype(jnp.float32) + router_term
    ).astype(jnp.bfloat16)
    router_part = jnp.dot(tokens.astype(jnp.float32).T, dense_grad, precision=lax.Precision.HIGHEST)
    grad_router = ctx_sum(router_part)
    return (mixed, grad_tokens, grad_router, grad_gate, grad_up, grad_down)


def solution(mesh):
    placed = (
        P("ctx", "head"),
        P("ctx", "head"),
        P("ctx", None),
        P("head", None),
        P("ctx", None, "head"),
        P("ctx", None, "head"),
        P("ctx", None, "head"),
    )
    return jax.shard_map(
        local,
        mesh=mesh,
        in_specs=placed,
        out_specs=(
            P("ctx", "head"),
            P("ctx", "head"),
            P("head", None),
            P("ctx", None, "head"),
            P("ctx", None, "head"),
            P("ctx", None, "head"),
        ),
        check_vma=False,
    )
```

```python
import jax
import jax.numpy as jnp
from jax import lax
from jax.sharding import PartitionSpec as P


def contract_rows(left, right):
    return lax.dot_general(
        left, right, (((0,), (0,)), ((), ())), preferred_element_type=jnp.float32
    )


def contract_last(left, right):
    return lax.dot_general(
        left, right, (((1,), (1,)), ((), ())), preferred_element_type=jnp.float32
    )


def forward_act(gate_pre, up_pre):
    sigma = jax.nn.sigmoid(gate_pre)
    active = gate_pre * sigma
    return (active * up_pre).astype(jnp.bfloat16)


def backward_act(gate_pre, up_pre, back_proj, prob_rows):
    sigma = jax.nn.sigmoid(gate_pre)
    active = gate_pre * sigma
    hidden_grad = prob_rows[:, None] * back_proj
    gate_grad = (hidden_grad * up_pre * sigma * (1.0 + gate_pre * (1.0 - sigma))).astype(
        jnp.bfloat16
    )
    up_grad = (hidden_grad * active).astype(jnp.bfloat16)
    return (gate_grad, up_grad)


def head_sum(part):
    count = lax.axis_size("head")
    spread = jnp.broadcast_to(part[None], (count,) + part.shape)
    gathered = lax.all_to_all(spread, "head", split_axis=0, concat_axis=0, tiled=True)
    return jnp.sum(gathered, axis=0)


def ctx_sum(part):
    count = lax.axis_size("ctx")
    rows = part.shape[0]
    pieces = part.reshape(count, rows // count, part.shape[1])
    mine = jnp.sum(lax.all_to_all(pieces, "ctx", split_axis=0, concat_axis=0, tiled=True), axis=0)
    spread = jnp.broadcast_to(mine[None], pieces.shape)
    return lax.all_to_all(spread, "ctx", split_axis=0, concat_axis=0, tiled=True).reshape(part.shape)


def local(tokens, cotangent, expert_ids, w_router, w_gate, w_up, w_down):
    ctx_count = lax.axis_size("ctx")
    tok_rows = tokens.shape[0]
    shard_width = tokens.shape[1]
    pick_count = expert_ids.shape[1]
    experts = w_router.shape[1]
    capacity = 3 * tok_rows * pick_count // (2 * experts)
    partial_logits = jnp.dot(tokens, w_router, preferred_element_type=jnp.float32)
    onehot = (expert_ids[:, :, None] == jnp.arange(experts, dtype=jnp.int32)[None, None, :]).astype(
        jnp.float32
    )
    chosen = head_sum(jnp.sum(partial_logits[:, None, :] * onehot, axis=2))
    prob_pairs = jnp.stack(
        [jax.nn.sigmoid(chosen[:, 0] - chosen[:, 1]), jax.nn.sigmoid(chosen[:, 1] - chosen[:, 0])],
        axis=1,
    )
    flat_ids = expert_ids.reshape(-1)
    id_hits = (flat_ids[:, None] == jnp.arange(experts, dtype=jnp.int32)[None, :]).astype(jnp.int32)
    places = jnp.sum((jnp.cumsum(id_hits, axis=0) - 1) * id_hits, axis=1)
    slot_index = flat_ids * capacity + places
    slot_table = (
        jnp.zeros((experts * capacity,), jnp.int32)
        .at[slot_index]
        .set(jnp.arange(tok_rows * pick_count, dtype=jnp.int32) + 1)
    )
    occupied = slot_table > 0
    source = jnp.maximum(slot_table - 1, 0)
    row_index = source // pick_count
    prob_send = jnp.where(occupied, prob_pairs.reshape(-1)[source], jnp.float32(0.0)).reshape(
        experts, capacity
    )

    def pack_rows(values):
        picked = jnp.where(occupied[:, None], values[row_index], jnp.zeros((), values.dtype))
        return picked.reshape(experts, capacity, values.shape[1])

    pad = jnp.zeros((experts, capacity, 128), jnp.bfloat16)
    cot_pack = jnp.concatenate(
        [pack_rows(cotangent), pad.at[:, :, 0].set(prob_send.astype(jnp.bfloat16))], axis=2
    )
    recv_x = lax.all_to_all(pack_rows(tokens), "ctx", split_axis=0, concat_axis=0, tiled=True)
    recv_g = lax.all_to_all(cot_pack, "ctx", split_axis=0, concat_axis=0, tiled=True)
    slot_count = recv_x.shape[0] * recv_x.shape[1]
    x_rows = recv_x.reshape(slot_count, shard_width)
    cot_rows = recv_g[:, :, :shard_width].reshape(slot_count, shard_width)
    prob_rows = recv_g[:, :, shard_width].reshape(slot_count).astype(jnp.float32)
    gate_w = w_gate[0]
    up_w = w_up[0]
    down_w = w_down[0]
    gate_part = contract_last(x_rows, gate_w).astype(jnp.bfloat16)
    up_part = contract_last(x_rows, up_w).astype(jnp.bfloat16)
    gate_sum, up_sum = lax.psum((gate_part, up_part), "head")
    back_part = contract_last(cot_rows, down_w).astype(jnp.bfloat16)
    back_part, gate_sum, up_sum = lax.optimization_barrier((back_part, gate_sum, up_sum))
    back_sum = lax.psum(back_part, "head")
    hidden = forward_act(gate_sum.astype(jnp.float32), up_sum.astype(jnp.float32))
    out_rows = jnp.dot(hidden, down_w, preferred_element_type=jnp.float32).astype(jnp.bfloat16)
    gate_late, up_late, back_sum = lax.optimization_barrier((gate_sum, up_sum, back_sum))
    gate_grad, up_grad = backward_act(
        gate_late.astype(jnp.float32),
        up_late.astype(jnp.float32),
        back_sum.astype(jnp.float32),
        prob_rows,
    )
    dx_rows = (
        jnp.dot(gate_grad, gate_w, preferred_element_type=jnp.float32)
        + jnp.dot(up_grad, up_w, preferred_element_type=jnp.float32)
    ).astype(jnp.bfloat16)
    hidden_kept = lax.optimization_barrier(hidden)
    scaled = (prob_rows[:, None] * hidden_kept.astype(jnp.float32)).astype(jnp.bfloat16)
    grad_down = contract_rows(scaled, cot_rows).astype(jnp.bfloat16)[None]
    grad_gate = contract_rows(gate_grad, x_rows).astype(jnp.bfloat16)[None]
    grad_up = contract_rows(up_grad, x_rows).astype(jnp.bfloat16)[None]
    back_out, back_dx = (
        lax.all_to_all(
            out_rows.reshape(ctx_count, capacity, shard_width),
            "ctx",
            split_axis=0,
            concat_axis=0,
            tiled=True,
        ),
        lax.all_to_all(
            dx_rows.reshape(ctx_count, capacity, shard_width),
            "ctx",
            split_axis=0,
            concat_axis=0,
            tiled=True,
        ),
    )
    out_pairs = back_out.reshape(experts * capacity, shard_width)[slot_index].reshape(
        tok_rows, pick_count, shard_width
    )
    dx_pairs = back_dx.reshape(experts * capacity, shard_width)[slot_index].reshape(
        tok_rows, pick_count, shard_width
    )
    mixed = jnp.sum(prob_pairs[:, :, None] * out_pairs.astype(jnp.float32), axis=1).astype(
        jnp.bfloat16
    )
    score_part = jnp.sum(
        cotangent.astype(jnp.float32)[:, None, :] * out_pairs.astype(jnp.float32), axis=2
    )
    score_grad = head_sum(score_part)
    logit_lead = prob_pairs[:, 0] * prob_pairs[:, 1] * (score_grad[:, 0] - score_grad[:, 1])
    logit_grad = jnp.stack([logit_lead, -logit_lead], axis=1)
    dense_grad = jnp.sum(logit_grad[:, :, None] * onehot, axis=1)
    router_term = jnp.dot(
        dense_grad, w_router.astype(jnp.float32).T, precision=lax.Precision.HIGHEST
    )
    grad_tokens = (
        dx_pairs[:, 0].astype(jnp.float32) + dx_pairs[:, 1].astype(jnp.float32) + router_term
    ).astype(jnp.bfloat16)
    router_part = jnp.dot(tokens.astype(jnp.float32).T, dense_grad, precision=lax.Precision.HIGHEST)
    grad_router = ctx_sum(router_part)
    return (mixed, grad_tokens, grad_router, grad_gate, grad_up, grad_down)


def solution(mesh):
    placed = (
        P("ctx", "head"),
        P("ctx", "head"),
        P("ctx", None),
        P("head", None),
        P("ctx", None, "head"),
        P("ctx", None, "head"),
        P("ctx", None, "head"),
    )
    return jax.shard_map(
        local,
        mesh=mesh,
        in_specs=placed,
        out_specs=(
            P("ctx", "head"),
            P("ctx", "head"),
            P("head", None),
            P("ctx", None, "head"),
            P("ctx", None, "head"),
            P("ctx", None, "head"),
        ),
        check_vma=False,
    )
```

```python
import jax
import jax.numpy as jnp
from jax import lax
from jax.sharding import PartitionSpec as P


def contract_rows(left, right):
    return lax.dot_general(
        left, right, (((0,), (0,)), ((), ())), preferred_element_type=jnp.float32
    )


def contract_last(left, right):
    return lax.dot_general(
        left, right, (((1,), (1,)), ((), ())), preferred_element_type=jnp.float32
    )


def forward_act(gate_pre, up_pre):
    sigma = jax.nn.sigmoid(gate_pre)
    active = gate_pre * sigma
    return (active * up_pre).astype(jnp.bfloat16)


def backward_act(gate_pre, up_pre, back_proj, prob_rows):
    sigma = jax.nn.sigmoid(gate_pre)
    active = gate_pre * sigma
    hidden_grad = prob_rows[:, None] * back_proj
    gate_grad = (hidden_grad * up_pre * sigma * (1.0 + gate_pre * (1.0 - sigma))).astype(
        jnp.bfloat16
    )
    up_grad = (hidden_grad * active).astype(jnp.bfloat16)
    return (gate_grad, up_grad)


def head_sum(part):
    count = lax.axis_size("head")
    spread = jnp.broadcast_to(part[None], (count,) + part.shape)
    gathered = lax.all_to_all(spread, "head", split_axis=0, concat_axis=0, tiled=True)
    return jnp.sum(gathered, axis=0)


def ctx_sum(part):
    count = lax.axis_size("ctx")
    rows = part.shape[0]
    pieces = part.reshape(count, rows // count, part.shape[1])
    mine = jnp.sum(lax.all_to_all(pieces, "ctx", split_axis=0, concat_axis=0, tiled=True), axis=0)
    spread = jnp.broadcast_to(mine[None], pieces.shape)
    return lax.all_to_all(spread, "ctx", split_axis=0, concat_axis=0, tiled=True).reshape(part.shape)


def local(tokens, cotangent, expert_ids, w_router, w_gate, w_up, w_down):
    ctx_count = lax.axis_size("ctx")
    tok_rows = tokens.shape[0]
    shard_width = tokens.shape[1]
    pick_count = expert_ids.shape[1]
    experts = w_router.shape[1]
    capacity = 3 * tok_rows * pick_count // (2 * experts)
    partial_logits = jnp.dot(tokens, w_router, preferred_element_type=jnp.float32)
    onehot = (expert_ids[:, :, None] == jnp.arange(experts, dtype=jnp.int32)[None, None, :]).astype(
        jnp.float32
    )
    chosen = head_sum(jnp.sum(partial_logits[:, None, :] * onehot, axis=2))
    prob_pairs = jnp.stack(
        [jax.nn.sigmoid(chosen[:, 0] - chosen[:, 1]), jax.nn.sigmoid(chosen[:, 1] - chosen[:, 0])],
        axis=1,
    )
    flat_ids = expert_ids.reshape(-1)
    id_hits = (flat_ids[:, None] == jnp.arange(experts, dtype=jnp.int32)[None, :]).astype(jnp.int32)
    places = jnp.sum((jnp.cumsum(id_hits, axis=0) - 1) * id_hits, axis=1)
    slot_index = flat_ids * capacity + places
    slot_table = (
        jnp.zeros((experts * capacity,), jnp.int32)
        .at[slot_index]
        .set(jnp.arange(tok_rows * pick_count, dtype=jnp.int32) + 1)
    )
    occupied = slot_table > 0
    source = jnp.maximum(slot_table - 1, 0)
    row_index = source // pick_count
    prob_send = jnp.where(occupied, prob_pairs.reshape(-1)[source], jnp.float32(0.0)).reshape(
        experts, capacity
    )

    def pack_rows(values):
        picked = jnp.where(occupied[:, None], values[row_index], jnp.zeros((), values.dtype))
        return picked.reshape(experts, capacity, values.shape[1])

    both = lax.all_to_all(
        jnp.concatenate([pack_rows(tokens), pack_rows(cotangent)], axis=2),
        "ctx",
        split_axis=0,
        concat_axis=0,
        tiled=True,
    )
    recv_p = lax.all_to_all(
        prob_send.astype(jnp.bfloat16), "ctx", split_axis=0, concat_axis=0, tiled=True
    )
    slot_count = both.shape[0] * both.shape[1]
    x_rows = both[:, :, :shard_width].reshape(slot_count, shard_width)
    cot_rows = both[:, :, shard_width:].reshape(slot_count, shard_width)
    prob_rows = recv_p.reshape(slot_count).astype(jnp.float32)
    gate_w = w_gate[0]
    up_w = w_up[0]
    down_w = w_down[0]
    gate_part = contract_last(x_rows, gate_w).astype(jnp.bfloat16)
    up_part = contract_last(x_rows, up_w).astype(jnp.bfloat16)
    back_part = contract_last(cot_rows, down_w).astype(jnp.bfloat16)
    gate_sum, up_sum, back_sum = lax.psum((gate_part, up_part, back_part), "head")
    gate_pre = gate_sum.astype(jnp.float32)
    up_pre = up_sum.astype(jnp.float32)
    hidden = forward_act(gate_pre, up_pre)
    gate_grad, up_grad = backward_act(gate_pre, up_pre, back_sum.astype(jnp.float32), prob_rows)
    out_rows = jnp.dot(hidden, down_w, preferred_element_type=jnp.float32).astype(jnp.bfloat16)
    dx_rows = (
        jnp.dot(gate_grad, gate_w, preferred_element_type=jnp.float32)
        + jnp.dot(up_grad, up_w, preferred_element_type=jnp.float32)
    ).astype(jnp.bfloat16)
    hidden_kept = lax.optimization_barrier(hidden)
    scaled = (prob_rows[:, None] * hidden_kept.astype(jnp.float32)).astype(jnp.bfloat16)
    grad_down = contract_rows(scaled, cot_rows).astype(jnp.bfloat16)[None]
    grad_gate = contract_rows(gate_grad, x_rows).astype(jnp.bfloat16)[None]
    grad_up = contract_rows(up_grad, x_rows).astype(jnp.bfloat16)[None]
    back_both = lax.all_to_all(
        jnp.concatenate([out_rows, dx_rows], axis=1).reshape(ctx_count, capacity, 2 * shard_width),
        "ctx",
        split_axis=0,
        concat_axis=0,
        tiled=True,
    )
    both_pairs = back_both.reshape(experts * capacity, 2 * shard_width)[slot_index].reshape(
        tok_rows, pick_count, 2 * shard_width
    )
    out_pairs = both_pairs[:, :, :shard_width]
    dx_pairs = both_pairs[:, :, shard_width:]
    mixed = jnp.sum(prob_pairs[:, :, None] * out_pairs.astype(jnp.float32), axis=1).astype(
        jnp.bfloat16
    )
    score_part = jnp.sum(
        cotangent.astype(jnp.float32)[:, None, :] * out_pairs.astype(jnp.float32), axis=2
    )
    score_grad = head_sum(score_part)
    logit_lead = prob_pairs[:, 0] * prob_pairs[:, 1] * (score_grad[:, 0] - score_grad[:, 1])
    logit_grad = jnp.stack([logit_lead, -logit_lead], axis=1)
    dense_grad = jnp.sum(logit_grad[:, :, None] * onehot, axis=1)
    router_term = jnp.dot(
        dense_grad, w_router.astype(jnp.float32).T, precision=lax.Precision.HIGHEST
    )
    grad_tokens = (
        dx_pairs[:, 0].astype(jnp.float32) + dx_pairs[:, 1].astype(jnp.float32) + router_term
    ).astype(jnp.bfloat16)
    router_part = jnp.dot(tokens.astype(jnp.float32).T, dense_grad, precision=lax.Precision.HIGHEST)
    grad_router = ctx_sum(router_part)
    return (mixed, grad_tokens, grad_router, grad_gate, grad_up, grad_down)


def solution(mesh):
    placed = (
        P("ctx", "head"),
        P("ctx", "head"),
        P("ctx", None),
        P("head", None),
        P("ctx", None, "head"),
        P("ctx", None, "head"),
        P("ctx", None, "head"),
    )
    return jax.shard_map(
        local,
        mesh=mesh,
        in_specs=placed,
        out_specs=(
            P("ctx", "head"),
            P("ctx", "head"),
            P("head", None),
            P("ctx", None, "head"),
            P("ctx", None, "head"),
            P("ctx", None, "head"),
        ),
        check_vma=False,
    )
```

```python
import jax
import jax.numpy as jnp
from jax import lax
from jax.sharding import PartitionSpec as P


def contract_rows(left, right):
    return lax.dot_general(
        left, right, (((0,), (0,)), ((), ())), preferred_element_type=jnp.float32
    )


def contract_last(left, right):
    return lax.dot_general(
        left, right, (((1,), (1,)), ((), ())), preferred_element_type=jnp.float32
    )


def forward_act(gate_pre, up_pre):
    sigma = jax.nn.sigmoid(gate_pre)
    active = gate_pre * sigma
    return (active * up_pre).astype(jnp.bfloat16)


def backward_act(gate_pre, up_pre, back_proj, prob_rows):
    sigma = jax.nn.sigmoid(gate_pre)
    active = gate_pre * sigma
    hidden_grad = prob_rows[:, None] * back_proj
    gate_grad = (hidden_grad * up_pre * sigma * (1.0 + gate_pre * (1.0 - sigma))).astype(
        jnp.bfloat16
    )
    up_grad = (hidden_grad * active).astype(jnp.bfloat16)
    return (gate_grad, up_grad)


def head_sum(part):
    count = lax.axis_size("head")
    spread = jnp.broadcast_to(part[None], (count,) + part.shape)
    gathered = lax.all_to_all(spread, "head", split_axis=0, concat_axis=0, tiled=True)
    return jnp.sum(gathered, axis=0)


def ctx_sum(part):
    count = lax.axis_size("ctx")
    rows = part.shape[0]
    pieces = part.reshape(count, rows // count, part.shape[1])
    mine = jnp.sum(lax.all_to_all(pieces, "ctx", split_axis=0, concat_axis=0, tiled=True), axis=0)
    spread = jnp.broadcast_to(mine[None], pieces.shape)
    return lax.all_to_all(spread, "ctx", split_axis=0, concat_axis=0, tiled=True).reshape(part.shape)


def local(tokens, cotangent, expert_ids, w_router, w_gate, w_up, w_down):
    ctx_count = lax.axis_size("ctx")
    tok_rows = tokens.shape[0]
    shard_width = tokens.shape[1]
    pick_count = expert_ids.shape[1]
    experts = w_router.shape[1]
    capacity = 3 * tok_rows * pick_count // (2 * experts)
    partial_logits = jnp.dot(tokens, w_router, preferred_element_type=jnp.float32)
    onehot = (expert_ids[:, :, None] == jnp.arange(experts, dtype=jnp.int32)[None, None, :]).astype(
        jnp.float32
    )
    chosen = head_sum(jnp.sum(partial_logits[:, None, :] * onehot, axis=2))
    prob_pairs = jnp.stack(
        [jax.nn.sigmoid(chosen[:, 0] - chosen[:, 1]), jax.nn.sigmoid(chosen[:, 1] - chosen[:, 0])],
        axis=1,
    )
    flat_ids = expert_ids.reshape(-1)
    id_hits = (flat_ids[:, None] == jnp.arange(experts, dtype=jnp.int32)[None, :]).astype(jnp.int32)
    places = jnp.sum((jnp.cumsum(id_hits, axis=0) - 1) * id_hits, axis=1)
    slot_index = flat_ids * capacity + places
    slot_ids = jnp.arange(experts * capacity, dtype=jnp.int32)
    pick_hit = slot_ids[:, None] == slot_index[None, :]
    token_hit = pick_hit.reshape(experts * capacity, tok_rows, pick_count).any(axis=2)
    rows_in = jnp.concatenate([tokens, cotangent], axis=1)
    packed = jnp.dot(
        token_hit.astype(jnp.bfloat16), rows_in, preferred_element_type=jnp.float32
    ).astype(jnp.bfloat16)
    prob_send = jnp.sum(jnp.where(pick_hit, prob_pairs.reshape(-1)[None, :], 0.0), axis=1)
    both = lax.all_to_all(
        packed.reshape(experts, capacity, 2 * shard_width),
        "ctx",
        split_axis=0,
        concat_axis=0,
        tiled=True,
    )
    recv_p = lax.all_to_all(
        prob_send.astype(jnp.bfloat16).reshape(experts, capacity),
        "ctx",
        split_axis=0,
        concat_axis=0,
        tiled=True,
    )
    slot_count = both.shape[0] * both.shape[1]
    x_rows = both[:, :, :shard_width].reshape(slot_count, shard_width)
    cot_rows = both[:, :, shard_width:].reshape(slot_count, shard_width)
    prob_rows = recv_p.reshape(slot_count).astype(jnp.float32)
    gate_w = w_gate[0]
    up_w = w_up[0]
    down_w = w_down[0]
    gate_part = contract_last(x_rows, gate_w).astype(jnp.bfloat16)
    up_part = contract_last(x_rows, up_w).astype(jnp.bfloat16)
    back_part = contract_last(cot_rows, down_w).astype(jnp.bfloat16)
    gate_sum, up_sum, back_sum = lax.psum((gate_part, up_part, back_part), "head")
    gate_pre = gate_sum.astype(jnp.float32)
    up_pre = up_sum.astype(jnp.float32)
    hidden = forward_act(gate_pre, up_pre)
    gate_grad, up_grad = backward_act(gate_pre, up_pre, back_sum.astype(jnp.float32), prob_rows)
    out_rows = jnp.dot(hidden, down_w, preferred_element_type=jnp.float32).astype(jnp.bfloat16)
    dx_rows = (
        jnp.dot(gate_grad, gate_w, preferred_element_type=jnp.float32)
        + jnp.dot(up_grad, up_w, preferred_element_type=jnp.float32)
    ).astype(jnp.bfloat16)
    hidden_kept = lax.optimization_barrier(hidden)
    scaled = (prob_rows[:, None] * hidden_kept.astype(jnp.float32)).astype(jnp.bfloat16)
    grad_down = contract_rows(scaled, cot_rows).astype(jnp.bfloat16)[None]
    grad_gate = contract_rows(gate_grad, x_rows).astype(jnp.bfloat16)[None]
    grad_up = contract_rows(up_grad, x_rows).astype(jnp.bfloat16)[None]
    back_both = lax.all_to_all(
        jnp.concatenate([out_rows, dx_rows], axis=1).reshape(ctx_count, capacity, 2 * shard_width),
        "ctx",
        split_axis=0,
        concat_axis=0,
        tiled=True,
    )
    both_pairs = lax.dot_general(
        pick_hit.astype(jnp.bfloat16),
        back_both.reshape(experts * capacity, 2 * shard_width),
        (((0,), (0,)), ((), ())),
        preferred_element_type=jnp.float32,
    ).astype(jnp.bfloat16).reshape(tok_rows, pick_count, 2 * shard_width)
    out_pairs = both_pairs[:, :, :shard_width]
    dx_pairs = both_pairs[:, :, shard_width:]
    mixed = jnp.sum(prob_pairs[:, :, None] * out_pairs.astype(jnp.float32), axis=1).astype(
        jnp.bfloat16
    )
    score_part = jnp.sum(
        cotangent.astype(jnp.float32)[:, None, :] * out_pairs.astype(jnp.float32), axis=2
    )
    score_grad = head_sum(score_part)
    logit_lead = prob_pairs[:, 0] * prob_pairs[:, 1] * (score_grad[:, 0] - score_grad[:, 1])
    logit_grad = jnp.stack([logit_lead, -logit_lead], axis=1)
    dense_grad = jnp.sum(logit_grad[:, :, None] * onehot, axis=1)
    router_term = jnp.dot(
        dense_grad, w_router.astype(jnp.float32).T, precision=lax.Precision.HIGHEST
    )
    grad_tokens = (
        dx_pairs[:, 0].astype(jnp.float32) + dx_pairs[:, 1].astype(jnp.float32) + router_term
    ).astype(jnp.bfloat16)
    router_part = jnp.dot(tokens.astype(jnp.float32).T, dense_grad, precision=lax.Precision.HIGHEST)
    grad_router = ctx_sum(router_part)
    return (mixed, grad_tokens, grad_router, grad_gate, grad_up, grad_down)


def solution(mesh):
    placed = (
        P("ctx", "head"),
        P("ctx", "head"),
        P("ctx", None),
        P("head", None),
        P("ctx", None, "head"),
        P("ctx", None, "head"),
        P("ctx", None, "head"),
    )
    return jax.shard_map(
        local,
        mesh=mesh,
        in_specs=placed,
        out_specs=(
            P("ctx", "head"),
            P("ctx", "head"),
            P("head", None),
            P("ctx", None, "head"),
            P("ctx", None, "head"),
            P("ctx", None, "head"),
        ),
        check_vma=False,
    )
```

```python
import jax
import jax.numpy as jnp
from jax import lax
from jax.sharding import PartitionSpec as P


def contract_rows(left, right):
    return lax.dot_general(
        left, right, (((0,), (0,)), ((), ())), preferred_element_type=jnp.float32
    )


def contract_last(left, right):
    return lax.dot_general(
        left, right, (((1,), (1,)), ((), ())), preferred_element_type=jnp.float32
    )


def forward_act(gate_pre, up_pre):
    sigma = jax.nn.sigmoid(gate_pre)
    active = gate_pre * sigma
    return (active * up_pre).astype(jnp.bfloat16)


def backward_act(gate_pre, up_pre, back_proj, prob_rows):
    sigma = jax.nn.sigmoid(gate_pre)
    active = gate_pre * sigma
    hidden_grad = prob_rows[:, None] * back_proj
    gate_grad = (hidden_grad * up_pre * sigma * (1.0 + gate_pre * (1.0 - sigma))).astype(
        jnp.bfloat16
    )
    up_grad = (hidden_grad * active).astype(jnp.bfloat16)
    return (gate_grad, up_grad)


def head_sum(part):
    count = lax.axis_size("head")
    spread = jnp.broadcast_to(part[None], (count,) + part.shape)
    gathered = lax.all_to_all(spread, "head", split_axis=0, concat_axis=0, tiled=True)
    return jnp.sum(gathered, axis=0)


def ctx_sum(part):
    count = lax.axis_size("ctx")
    rows = part.shape[0]
    pieces = part.reshape(count, rows // count, part.shape[1])
    mine = jnp.sum(lax.all_to_all(pieces, "ctx", split_axis=0, concat_axis=0, tiled=True), axis=0)
    spread = jnp.broadcast_to(mine[None], pieces.shape)
    return lax.all_to_all(spread, "ctx", split_axis=0, concat_axis=0, tiled=True).reshape(part.shape)


def local(tokens, cotangent, expert_ids, w_router, w_gate, w_up, w_down):
    ctx_count = lax.axis_size("ctx")
    tok_rows = tokens.shape[0]
    shard_width = tokens.shape[1]
    pick_count = expert_ids.shape[1]
    experts = w_router.shape[1]
    capacity = 3 * tok_rows * pick_count // (2 * experts)
    partial_logits = jnp.dot(tokens, w_router, preferred_element_type=jnp.float32)
    onehot = (expert_ids[:, :, None] == jnp.arange(experts, dtype=jnp.int32)[None, None, :]).astype(
        jnp.float32
    )
    chosen = head_sum(jnp.sum(partial_logits[:, None, :] * onehot, axis=2))
    prob_pairs = jnp.stack(
        [jax.nn.sigmoid(chosen[:, 0] - chosen[:, 1]), jax.nn.sigmoid(chosen[:, 1] - chosen[:, 0])],
        axis=1,
    )
    flat_ids = expert_ids.reshape(-1)
    id_hits = (flat_ids[:, None] == jnp.arange(experts, dtype=jnp.int32)[None, :]).astype(jnp.int32)
    places = jnp.sum((jnp.cumsum(id_hits, axis=0) - 1) * id_hits, axis=1)
    slot_index = flat_ids * capacity + places
    slot_ids = jnp.arange(experts * capacity, dtype=jnp.int32)
    pick_hit = slot_ids[:, None] == slot_index[None, :]
    token_hit = pick_hit.reshape(experts * capacity, tok_rows, pick_count).any(axis=2)
    rows_in = jnp.concatenate([tokens, cotangent], axis=1)
    packed = jnp.dot(
        token_hit.astype(jnp.bfloat16), rows_in, preferred_element_type=jnp.float32
    ).astype(jnp.bfloat16)
    pair_prod = prob_pairs[:, 0] * prob_pairs[:, 1]
    q_hi = pair_prod.astype(jnp.bfloat16).astype(jnp.float32)
    q_lo = pair_prod - q_hi
    pick_values = jnp.stack(
        [
            prob_pairs.reshape(-1),
            jnp.repeat(q_hi, pick_count),
            jnp.repeat(q_lo, pick_count),
            expert_ids[:, ::-1].reshape(-1).astype(jnp.float32),
        ],
        axis=0,
    )
    slot_values = jnp.sum(
        jnp.where(pick_hit[None], pick_values[:, None, :], 0.0), axis=2
    ).astype(jnp.bfloat16)
    both = lax.all_to_all(
        packed.reshape(experts, capacity, 2 * shard_width),
        "ctx",
        split_axis=0,
        concat_axis=0,
        tiled=True,
    )
    recv_p = lax.all_to_all(
        slot_values.reshape(4, experts, capacity).transpose(1, 0, 2),
        "ctx",
        split_axis=0,
        concat_axis=0,
        tiled=True,
    )
    slot_count = both.shape[0] * both.shape[1]
    x_rows = both[:, :, :shard_width].reshape(slot_count, shard_width)
    cot_rows = both[:, :, shard_width:].reshape(slot_count, shard_width)
    row_values = recv_p.transpose(1, 0, 2).reshape(4, slot_count).astype(jnp.float32)
    prob_rows = row_values[0]
    pair_rows = row_values[1] + row_values[2]
    other_rows = row_values[3].astype(jnp.int32)
    gate_w = w_gate[0]
    up_w = w_up[0]
    down_w = w_down[0]
    gate_part = contract_last(x_rows, gate_w).astype(jnp.bfloat16)
    up_part = contract_last(x_rows, up_w).astype(jnp.bfloat16)
    back_part = contract_last(cot_rows, down_w).astype(jnp.bfloat16)
    gate_sum, up_sum, back_sum = lax.psum((gate_part, up_part, back_part), "head")
    gate_pre = gate_sum.astype(jnp.float32)
    up_pre = up_sum.astype(jnp.float32)
    hidden = forward_act(gate_pre, up_pre)
    gate_grad, up_grad = backward_act(gate_pre, up_pre, back_sum.astype(jnp.float32), prob_rows)
    out_rows = jnp.dot(hidden, down_w, preferred_element_type=jnp.float32).astype(jnp.bfloat16)
    dx_rows = (
        jnp.dot(gate_grad, gate_w, preferred_element_type=jnp.float32)
        + jnp.dot(up_grad, up_w, preferred_element_type=jnp.float32)
    ).astype(jnp.bfloat16)
    hidden_kept = lax.optimization_barrier(hidden)
    scaled = (prob_rows[:, None] * hidden_kept.astype(jnp.float32)).astype(jnp.bfloat16)
    grad_down = contract_rows(scaled, cot_rows).astype(jnp.bfloat16)[None]
    grad_gate = contract_rows(gate_grad, x_rows).astype(jnp.bfloat16)[None]
    grad_up = contract_rows(up_grad, x_rows).astype(jnp.bfloat16)[None]
    score_rows = head_sum(
        jnp.sum(cot_rows.astype(jnp.float32) * out_rows.astype(jnp.float32), axis=1)
    )
    own = lax.axis_index("ctx")
    expert_ids_row = jnp.arange(experts, dtype=jnp.int32)[None, :]
    direction = (expert_ids_row == own).astype(jnp.float32) - (
        expert_ids_row == other_rows[:, None]
    ).astype(jnp.float32)
    router_weight = (pair_rows * score_rows)[:, None] * direction
    router_part = jnp.dot(
        x_rows.astype(jnp.float32).T, router_weight, precision=lax.Precision.HIGHEST
    )
    s_hi = score_rows.astype(jnp.bfloat16)
    s_lo = (score_rows - s_hi.astype(jnp.float32)).astype(jnp.bfloat16)
    extra = jnp.zeros((slot_count, 128), jnp.bfloat16).at[:, 0].set(s_hi).at[:, 1].set(s_lo)
    back_both = lax.all_to_all(
        jnp.concatenate([out_rows, dx_rows, extra], axis=1).reshape(
            ctx_count, capacity, 2 * shard_width + 128
        ),
        "ctx",
        split_axis=0,
        concat_axis=0,
        tiled=True,
    )
    router_part, back_both = lax.optimization_barrier((router_part, back_both))
    grad_router = ctx_sum(router_part)
    both_pairs = lax.dot_general(
        pick_hit.astype(jnp.bfloat16),
        back_both.reshape(experts * capacity, 2 * shard_width + 128),
        (((0,), (0,)), ((), ())),
        preferred_element_type=jnp.float32,
    ).reshape(tok_rows, pick_count, 2 * shard_width + 128)
    out_pairs = both_pairs[:, :, :shard_width].astype(jnp.bfloat16)
    dx_pairs = both_pairs[:, :, shard_width : 2 * shard_width].astype(jnp.bfloat16)
    score_grad = both_pairs[:, :, 2 * shard_width] + both_pairs[:, :, 2 * shard_width + 1]
    mixed = jnp.sum(prob_pairs[:, :, None] * out_pairs.astype(jnp.float32), axis=1).astype(
        jnp.bfloat16
    )
    logit_lead = prob_pairs[:, 0] * prob_pairs[:, 1] * (score_grad[:, 0] - score_grad[:, 1])
    logit_grad = jnp.stack([logit_lead, -logit_lead], axis=1)
    dense_grad = jnp.sum(logit_grad[:, :, None] * onehot, axis=1)
    router_term = jnp.dot(
        dense_grad, w_router.astype(jnp.float32).T, precision=lax.Precision.HIGHEST
    )
    grad_tokens = (
        dx_pairs[:, 0].astype(jnp.float32) + dx_pairs[:, 1].astype(jnp.float32) + router_term
    ).astype(jnp.bfloat16)
    return (mixed, grad_tokens, grad_router, grad_gate, grad_up, grad_down)


def solution(mesh):
    placed = (
        P("ctx", "head"),
        P("ctx", "head"),
        P("ctx", None),
        P("head", None),
        P("ctx", None, "head"),
        P("ctx", None, "head"),
        P("ctx", None, "head"),
    )
    return jax.shard_map(
        local,
        mesh=mesh,
        in_specs=placed,
        out_specs=(
            P("ctx", "head"),
            P("ctx", "head"),
            P("head", None),
            P("ctx", None, "head"),
            P("ctx", None, "head"),
            P("ctx", None, "head"),
        ),
        check_vma=False,
    )
```

```python
import jax
import jax.numpy as jnp
from jax import lax
from jax.sharding import PartitionSpec as P


def contract_rows(left, right):
    return lax.dot_general(
        left, right, (((0,), (0,)), ((), ())), preferred_element_type=jnp.float32
    )


def contract_last(left, right):
    return lax.dot_general(
        left, right, (((1,), (1,)), ((), ())), preferred_element_type=jnp.float32
    )


def forward_act(gate_pre, up_pre):
    sigma = jax.nn.sigmoid(gate_pre)
    active = gate_pre * sigma
    return (active * up_pre).astype(jnp.bfloat16)


def backward_act(gate_pre, up_pre, back_proj, prob_rows):
    sigma = jax.nn.sigmoid(gate_pre)
    active = gate_pre * sigma
    hidden_grad = prob_rows[:, None] * back_proj
    gate_grad = (hidden_grad * up_pre * sigma * (1.0 + gate_pre * (1.0 - sigma))).astype(
        jnp.bfloat16
    )
    up_grad = (hidden_grad * active).astype(jnp.bfloat16)
    return (gate_grad, up_grad)


def head_sum(part):
    count = lax.axis_size("head")
    spread = jnp.broadcast_to(part[None], (count,) + part.shape)
    gathered = lax.all_to_all(spread, "head", split_axis=0, concat_axis=0, tiled=True)
    return jnp.sum(gathered, axis=0)


def ctx_sum(part):
    count = lax.axis_size("ctx")
    rows = part.shape[0]
    pieces = part.reshape(count, rows // count, part.shape[1])
    mine = jnp.sum(lax.all_to_all(pieces, "ctx", split_axis=0, concat_axis=0, tiled=True), axis=0)
    spread = jnp.broadcast_to(mine[None], pieces.shape)
    return lax.all_to_all(spread, "ctx", split_axis=0, concat_axis=0, tiled=True).reshape(part.shape)


def local(tokens, cotangent, expert_ids, w_router, w_gate, w_up, w_down):
    ctx_count = lax.axis_size("ctx")
    tok_rows = tokens.shape[0]
    shard_width = tokens.shape[1]
    pick_count = expert_ids.shape[1]
    experts = w_router.shape[1]
    capacity = 3 * tok_rows * pick_count // (2 * experts)
    partial_logits = jnp.dot(tokens, w_router, preferred_element_type=jnp.float32)
    onehot = (expert_ids[:, :, None] == jnp.arange(experts, dtype=jnp.int32)[None, None, :]).astype(
        jnp.float32
    )
    chosen = head_sum(jnp.sum(partial_logits[:, None, :] * onehot, axis=2))
    prob_pairs = jnp.stack(
        [jax.nn.sigmoid(chosen[:, 0] - chosen[:, 1]), jax.nn.sigmoid(chosen[:, 1] - chosen[:, 0])],
        axis=1,
    )
    flat_ids = expert_ids.reshape(-1)
    id_hits = (flat_ids[:, None] == jnp.arange(experts, dtype=jnp.int32)[None, :]).astype(jnp.int32)
    places = jnp.sum((jnp.cumsum(id_hits, axis=0) - 1) * id_hits, axis=1)
    slot_index = flat_ids * capacity + places
    slot_ids = jnp.arange(experts * capacity, dtype=jnp.int32)
    pick_hit = slot_ids[:, None] == slot_index[None, :]
    token_hit = pick_hit.reshape(experts * capacity, tok_rows, pick_count).any(axis=2)
    rows_in = jnp.concatenate([tokens, cotangent], axis=1)
    packed = jnp.dot(
        token_hit.astype(jnp.bfloat16), rows_in, preferred_element_type=jnp.float32
    ).astype(jnp.bfloat16)
    pair_prod = prob_pairs[:, 0] * prob_pairs[:, 1]
    q_hi = pair_prod.astype(jnp.bfloat16).astype(jnp.float32)
    q_lo = pair_prod - q_hi
    pick_values = jnp.stack(
        [
            prob_pairs.reshape(-1),
            jnp.repeat(q_hi, pick_count),
            jnp.repeat(q_lo, pick_count),
            expert_ids[:, ::-1].reshape(-1).astype(jnp.float32),
        ],
        axis=0,
    )
    slot_values = jnp.sum(
        jnp.where(pick_hit[None], pick_values[:, None, :], 0.0), axis=2
    ).astype(jnp.bfloat16)
    both = lax.all_to_all(
        packed.reshape(experts, capacity, 2 * shard_width),
        "ctx",
        split_axis=0,
        concat_axis=0,
        tiled=True,
    )
    recv_p = lax.all_to_all(
        slot_values.reshape(4, experts, capacity).transpose(1, 0, 2),
        "ctx",
        split_axis=0,
        concat_axis=0,
        tiled=True,
    )
    slot_count = both.shape[0] * both.shape[1]
    x_rows = both[:, :, :shard_width].reshape(slot_count, shard_width)
    cot_rows = both[:, :, shard_width:].reshape(slot_count, shard_width)
    row_values = recv_p.transpose(1, 0, 2).reshape(4, slot_count).astype(jnp.float32)
    prob_rows = row_values[0]
    pair_rows = row_values[1] + row_values[2]
    other_rows = row_values[3].astype(jnp.int32)
    gate_w = w_gate[0]
    up_w = w_up[0]
    down_w = w_down[0]
    gate_part = contract_last(x_rows, gate_w).astype(jnp.bfloat16)
    up_part = contract_last(x_rows, up_w).astype(jnp.bfloat16)
    back_part = contract_last(cot_rows, down_w).astype(jnp.bfloat16)
    gate_sum, up_sum, back_sum = lax.psum((gate_part, up_part, back_part), "head")
    gate_pre = gate_sum.astype(jnp.float32)
    up_pre = up_sum.astype(jnp.float32)
    hidden = forward_act(gate_pre, up_pre)
    back_proj = back_sum.astype(jnp.float32)
    gate_grad, up_grad = backward_act(gate_pre, up_pre, back_proj, prob_rows)
    out_rows = jnp.dot(hidden, down_w, preferred_element_type=jnp.float32).astype(jnp.bfloat16)
    dx_rows = (
        jnp.dot(gate_grad, gate_w, preferred_element_type=jnp.float32)
        + jnp.dot(up_grad, up_w, preferred_element_type=jnp.float32)
    ).astype(jnp.bfloat16)
    hidden_kept = lax.optimization_barrier(hidden)
    scaled = (prob_rows[:, None] * hidden_kept.astype(jnp.float32)).astype(jnp.bfloat16)
    grad_down = contract_rows(scaled, cot_rows).astype(jnp.bfloat16)[None]
    grad_gate = contract_rows(gate_grad, x_rows).astype(jnp.bfloat16)[None]
    grad_up = contract_rows(up_grad, x_rows).astype(jnp.bfloat16)[None]
    score_rows = jnp.sum(hidden.astype(jnp.float32) * back_proj, axis=1)
    own = lax.axis_index("ctx")
    expert_ids_row = jnp.arange(experts, dtype=jnp.int32)[None, :]
    direction = (expert_ids_row == own).astype(jnp.float32) - (
        expert_ids_row == other_rows[:, None]
    ).astype(jnp.float32)
    router_weight = (pair_rows * score_rows)[:, None] * direction
    router_part = jnp.dot(
        x_rows.astype(jnp.float32).T, router_weight, precision=lax.Precision.HIGHEST
    )
    s_hi = score_rows.astype(jnp.bfloat16)
    s_lo = (score_rows - s_hi.astype(jnp.float32)).astype(jnp.bfloat16)
    extra = jnp.zeros((slot_count, 128), jnp.bfloat16).at[:, 0].set(s_hi).at[:, 1].set(s_lo)
    back_both = lax.all_to_all(
        jnp.concatenate([out_rows, dx_rows, extra], axis=1).reshape(
            ctx_count, capacity, 2 * shard_width + 128
        ),
        "ctx",
        split_axis=0,
        concat_axis=0,
        tiled=True,
    )
    grad_router = ctx_sum(router_part)
    both_pairs = lax.dot_general(
        pick_hit.astype(jnp.bfloat16),
        back_both.reshape(experts * capacity, 2 * shard_width + 128),
        (((0,), (0,)), ((), ())),
        preferred_element_type=jnp.float32,
    ).reshape(tok_rows, pick_count, 2 * shard_width + 128)
    out_pairs = both_pairs[:, :, :shard_width].astype(jnp.bfloat16)
    dx_pairs = both_pairs[:, :, shard_width : 2 * shard_width].astype(jnp.bfloat16)
    score_grad = both_pairs[:, :, 2 * shard_width] + both_pairs[:, :, 2 * shard_width + 1]
    mixed = jnp.sum(prob_pairs[:, :, None] * out_pairs.astype(jnp.float32), axis=1).astype(
        jnp.bfloat16
    )
    logit_lead = prob_pairs[:, 0] * prob_pairs[:, 1] * (score_grad[:, 0] - score_grad[:, 1])
    logit_grad = jnp.stack([logit_lead, -logit_lead], axis=1)
    dense_grad = jnp.sum(logit_grad[:, :, None] * onehot, axis=1)
    router_term = jnp.dot(
        dense_grad, w_router.astype(jnp.float32).T, precision=lax.Precision.HIGHEST
    )
    grad_tokens = (
        dx_pairs[:, 0].astype(jnp.float32) + dx_pairs[:, 1].astype(jnp.float32) + router_term
    ).astype(jnp.bfloat16)
    return (mixed, grad_tokens, grad_router, grad_gate, grad_up, grad_down)


def solution(mesh):
    placed = (
        P("ctx", "head"),
        P("ctx", "head"),
        P("ctx", None),
        P("head", None),
        P("ctx", None, "head"),
        P("ctx", None, "head"),
        P("ctx", None, "head"),
    )
    return jax.shard_map(
        local,
        mesh=mesh,
        in_specs=placed,
        out_specs=(
            P("ctx", "head"),
            P("ctx", "head"),
            P("head", None),
            P("ctx", None, "head"),
            P("ctx", None, "head"),
            P("ctx", None, "head"),
        ),
        check_vma=False,
    )
```

```python
import jax
import jax.numpy as jnp
from jax import lax
from jax.sharding import PartitionSpec as P


def contract_rows(left, right):
    return lax.dot_general(
        left, right, (((0,), (0,)), ((), ())), preferred_element_type=jnp.float32
    )


def contract_last(left, right):
    return lax.dot_general(
        left, right, (((1,), (1,)), ((), ())), preferred_element_type=jnp.float32
    )


def forward_act(gate_pre, up_pre):
    sigma = jax.nn.sigmoid(gate_pre)
    active = gate_pre * sigma
    return (active * up_pre).astype(jnp.bfloat16)


def backward_act(gate_pre, up_pre, back_proj, prob_rows):
    sigma = jax.nn.sigmoid(gate_pre)
    active = gate_pre * sigma
    hidden_grad = prob_rows[:, None] * back_proj
    gate_grad = (hidden_grad * up_pre * sigma * (1.0 + gate_pre * (1.0 - sigma))).astype(
        jnp.bfloat16
    )
    up_grad = (hidden_grad * active).astype(jnp.bfloat16)
    return (gate_grad, up_grad)


def head_sum(part):
    count = lax.axis_size("head")
    spread = jnp.broadcast_to(part[None], (count,) + part.shape)
    gathered = lax.all_to_all(spread, "head", split_axis=0, concat_axis=0, tiled=True)
    return jnp.sum(gathered, axis=0)


def ctx_sum(part):
    count = lax.axis_size("ctx")
    rows = part.shape[0]
    pieces = part.reshape(count, rows // count, part.shape[1])
    mine = jnp.sum(lax.all_to_all(pieces, "ctx", split_axis=0, concat_axis=0, tiled=True), axis=0)
    spread = jnp.broadcast_to(mine[None], pieces.shape)
    return lax.all_to_all(spread, "ctx", split_axis=0, concat_axis=0, tiled=True).reshape(part.shape)


def local(tokens, cotangent, expert_ids, w_router, w_gate, w_up, w_down):
    ctx_count = lax.axis_size("ctx")
    tok_rows = tokens.shape[0]
    shard_width = tokens.shape[1]
    pick_count = expert_ids.shape[1]
    experts = w_router.shape[1]
    capacity = 3 * tok_rows * pick_count // (2 * experts)
    partial_logits = jnp.dot(tokens, w_router, preferred_element_type=jnp.float32)
    onehot = (expert_ids[:, :, None] == jnp.arange(experts, dtype=jnp.int32)[None, None, :]).astype(
        jnp.float32
    )
    chosen = head_sum(jnp.sum(partial_logits[:, None, :] * onehot, axis=2))
    prob_pairs = jnp.stack(
        [jax.nn.sigmoid(chosen[:, 0] - chosen[:, 1]), jax.nn.sigmoid(chosen[:, 1] - chosen[:, 0])],
        axis=1,
    )
    flat_ids = expert_ids.reshape(-1)
    id_hits = (flat_ids[:, None] == jnp.arange(experts, dtype=jnp.int32)[None, :]).astype(jnp.int32)
    places = jnp.sum((jnp.cumsum(id_hits, axis=0) - 1) * id_hits, axis=1)
    slot_index = flat_ids * capacity + places
    slot_ids = jnp.arange(experts * capacity, dtype=jnp.int32)
    pick_hit = slot_ids[:, None] == slot_index[None, :]
    token_hit = pick_hit.reshape(experts * capacity, tok_rows, pick_count).any(axis=2)
    rows_in = jnp.concatenate([tokens, cotangent], axis=1)
    packed = jnp.dot(
        token_hit.astype(jnp.bfloat16), rows_in, preferred_element_type=jnp.float32
    ).astype(jnp.bfloat16)
    pair_prod = prob_pairs[:, 0] * prob_pairs[:, 1]
    q_hi = pair_prod.astype(jnp.bfloat16).astype(jnp.float32)
    q_lo = pair_prod - q_hi
    pick_values = jnp.stack(
        [
            prob_pairs.reshape(-1),
            jnp.repeat(q_hi, pick_count),
            jnp.repeat(q_lo, pick_count),
            expert_ids[:, ::-1].reshape(-1).astype(jnp.float32),
        ],
        axis=0,
    )
    slot_values = jnp.sum(
        jnp.where(pick_hit[None], pick_values[:, None, :], 0.0), axis=2
    ).astype(jnp.bfloat16)
    both = lax.all_to_all(
        packed.reshape(experts, capacity, 2 * shard_width),
        "ctx",
        split_axis=0,
        concat_axis=0,
        tiled=True,
    )
    recv_p = lax.all_to_all(
        slot_values.reshape(4, experts, capacity).transpose(1, 0, 2),
        "ctx",
        split_axis=0,
        concat_axis=0,
        tiled=True,
    )
    slot_count = both.shape[0] * both.shape[1]
    half = slot_count // 2
    swapped = lax.axis_index("head") % 2 == 1

    def local_order(rows):
        turned = jnp.concatenate([rows[half:], rows[:half]], axis=0)
        return jnp.where(swapped, turned, rows)

    both = local_order(both.reshape(slot_count, 2 * shard_width))
    x_rows = both[:, :shard_width]
    cot_rows = both[:, shard_width:]
    row_values = local_order(
        recv_p.transpose(0, 2, 1).reshape(slot_count, 4)
    ).T.astype(jnp.float32)
    prob_rows = row_values[0]
    pair_rows = row_values[1] + row_values[2]
    other_rows = row_values[3].astype(jnp.int32)
    gate_w = w_gate[0]
    up_w = w_up[0]
    down_w = w_down[0]
    gate_part = contract_last(x_rows, gate_w).astype(jnp.bfloat16)
    up_part = contract_last(x_rows, up_w).astype(jnp.bfloat16)
    back_part = contract_last(cot_rows, down_w).astype(jnp.bfloat16)
    head_count = lax.axis_size("head")
    partner = [(i, i ^ 1) for i in range(head_count)]
    same_core = [list(range(c, head_count, 2)) for c in range(2)]
    parts = jnp.stack([gate_part, up_part, back_part])
    pair_sum = (
        parts[:, :half].astype(jnp.float32)
        + lax.ppermute(parts[:, half:], "head", partner).astype(jnp.float32)
    ).astype(jnp.bfloat16)
    mine = lax.psum(pair_sum, "head", axis_index_groups=same_core)
    sums = jnp.concatenate([mine, lax.ppermute(mine, "head", partner)], axis=1)
    gate_sum, up_sum, back_sum = sums[0], sums[1], sums[2]
    gate_pre = gate_sum.astype(jnp.float32)
    up_pre = up_sum.astype(jnp.float32)
    hidden = forward_act(gate_pre, up_pre)
    back_proj = back_sum.astype(jnp.float32)
    gate_grad, up_grad = backward_act(gate_pre, up_pre, back_proj, prob_rows)
    out_rows = jnp.dot(hidden, down_w, preferred_element_type=jnp.float32).astype(jnp.bfloat16)
    dx_rows = (
        jnp.dot(gate_grad, gate_w, preferred_element_type=jnp.float32)
        + jnp.dot(up_grad, up_w, preferred_element_type=jnp.float32)
    ).astype(jnp.bfloat16)
    hidden_kept = lax.optimization_barrier(hidden)
    scaled = (prob_rows[:, None] * hidden_kept.astype(jnp.float32)).astype(jnp.bfloat16)
    grad_down = contract_rows(scaled, cot_rows).astype(jnp.bfloat16)[None]
    grad_gate = contract_rows(gate_grad, x_rows).astype(jnp.bfloat16)[None]
    grad_up = contract_rows(up_grad, x_rows).astype(jnp.bfloat16)[None]
    score_rows = jnp.sum(hidden.astype(jnp.float32) * back_proj, axis=1)
    own = lax.axis_index("ctx")
    expert_ids_row = jnp.arange(experts, dtype=jnp.int32)[None, :]
    direction = (expert_ids_row == own).astype(jnp.float32) - (
        expert_ids_row == other_rows[:, None]
    ).astype(jnp.float32)
    router_weight = (pair_rows * score_rows)[:, None] * direction
    router_part = jnp.dot(
        x_rows.astype(jnp.float32).T, router_weight, precision=lax.Precision.HIGHEST
    )
    s_hi = score_rows.astype(jnp.bfloat16)
    s_lo = (score_rows - s_hi.astype(jnp.float32)).astype(jnp.bfloat16)
    extra = jnp.zeros((slot_count, 128), jnp.bfloat16).at[:, 0].set(s_hi).at[:, 1].set(s_lo)
    back_both = lax.all_to_all(
        local_order(jnp.concatenate([out_rows, dx_rows, extra], axis=1)).reshape(
            ctx_count, capacity, 2 * shard_width + 128
        ),
        "ctx",
        split_axis=0,
        concat_axis=0,
        tiled=True,
    )
    grad_router = ctx_sum(router_part)
    both_pairs = lax.dot_general(
        pick_hit.astype(jnp.bfloat16),
        back_both.reshape(experts * capacity, 2 * shard_width + 128),
        (((0,), (0,)), ((), ())),
        preferred_element_type=jnp.float32,
    ).reshape(tok_rows, pick_count, 2 * shard_width + 128)
    out_pairs = both_pairs[:, :, :shard_width].astype(jnp.bfloat16)
    dx_pairs = both_pairs[:, :, shard_width : 2 * shard_width].astype(jnp.bfloat16)
    score_grad = both_pairs[:, :, 2 * shard_width] + both_pairs[:, :, 2 * shard_width + 1]
    mixed = jnp.sum(prob_pairs[:, :, None] * out_pairs.astype(jnp.float32), axis=1).astype(
        jnp.bfloat16
    )
    logit_lead = prob_pairs[:, 0] * prob_pairs[:, 1] * (score_grad[:, 0] - score_grad[:, 1])
    logit_grad = jnp.stack([logit_lead, -logit_lead], axis=1)
    dense_grad = jnp.sum(logit_grad[:, :, None] * onehot, axis=1)
    router_term = jnp.dot(
        dense_grad, w_router.astype(jnp.float32).T, precision=lax.Precision.HIGHEST
    )
    grad_tokens = (
        dx_pairs[:, 0].astype(jnp.float32) + dx_pairs[:, 1].astype(jnp.float32) + router_term
    ).astype(jnp.bfloat16)
    return (mixed, grad_tokens, grad_router, grad_gate, grad_up, grad_down)


def solution(mesh):
    placed = (
        P("ctx", "head"),
        P("ctx", "head"),
        P("ctx", None),
        P("head", None),
        P("ctx", None, "head"),
        P("ctx", None, "head"),
        P("ctx", None, "head"),
    )
    return jax.shard_map(
        local,
        mesh=mesh,
        in_specs=placed,
        out_specs=(
            P("ctx", "head"),
            P("ctx", "head"),
            P("head", None),
            P("ctx", None, "head"),
            P("ctx", None, "head"),
            P("ctx", None, "head"),
        ),
        check_vma=False,
    )
```

```python
import jax
import jax.numpy as jnp
from jax import lax
from jax.sharding import PartitionSpec as P


def contract_rows(left, right):
    return lax.dot_general(
        left, right, (((0,), (0,)), ((), ())), preferred_element_type=jnp.float32
    )


def contract_last(left, right):
    return lax.dot_general(
        left, right, (((1,), (1,)), ((), ())), preferred_element_type=jnp.float32
    )


def forward_act(gate_pre, up_pre):
    sigma = jax.nn.sigmoid(gate_pre)
    active = gate_pre * sigma
    return (active * up_pre).astype(jnp.bfloat16)


def backward_act(gate_pre, up_pre, back_proj, prob_rows):
    sigma = jax.nn.sigmoid(gate_pre)
    active = gate_pre * sigma
    hidden_grad = prob_rows[:, None] * back_proj
    gate_grad = (hidden_grad * up_pre * sigma * (1.0 + gate_pre * (1.0 - sigma))).astype(
        jnp.bfloat16
    )
    up_grad = (hidden_grad * active).astype(jnp.bfloat16)
    return (gate_grad, up_grad)


def head_sum(part):
    count = lax.axis_size("head")
    spread = jnp.broadcast_to(part[None], (count,) + part.shape)
    gathered = lax.all_to_all(spread, "head", split_axis=0, concat_axis=0, tiled=True)
    return jnp.sum(gathered, axis=0)


def ctx_sum(part):
    count = lax.axis_size("ctx")
    rows = part.shape[0]
    pieces = part.reshape(count, rows // count, part.shape[1])
    mine = jnp.sum(lax.all_to_all(pieces, "ctx", split_axis=0, concat_axis=0, tiled=True), axis=0)
    spread = jnp.broadcast_to(mine[None], pieces.shape)
    return lax.all_to_all(spread, "ctx", split_axis=0, concat_axis=0, tiled=True).reshape(part.shape)


def local(tokens, cotangent, expert_ids, w_router, w_gate, w_up, w_down):
    ctx_count = lax.axis_size("ctx")
    tok_rows = tokens.shape[0]
    shard_width = tokens.shape[1]
    pick_count = expert_ids.shape[1]
    experts = w_router.shape[1]
    capacity = 3 * tok_rows * pick_count // (2 * experts)
    partial_logits = jnp.dot(tokens, w_router, preferred_element_type=jnp.float32)
    onehot = (expert_ids[:, :, None] == jnp.arange(experts, dtype=jnp.int32)[None, None, :]).astype(
        jnp.float32
    )
    chosen_part = jnp.sum(partial_logits[:, None, :] * onehot, axis=2)
    flat_ids = expert_ids.reshape(-1)
    id_hits = (flat_ids[:, None] == jnp.arange(experts, dtype=jnp.int32)[None, :]).astype(jnp.int32)
    places = jnp.sum((jnp.cumsum(id_hits, axis=0) - 1) * id_hits, axis=1)
    slot_index = flat_ids * capacity + places
    slot_ids = jnp.arange(experts * capacity, dtype=jnp.int32)
    pick_hit = slot_ids[:, None] == slot_index[None, :]
    token_hit = pick_hit.reshape(experts * capacity, tok_rows, pick_count).any(axis=2)
    rows_in = jnp.concatenate([tokens, cotangent], axis=1)
    packed = jnp.dot(
        token_hit.astype(jnp.bfloat16), rows_in, preferred_element_type=jnp.float32
    ).astype(jnp.bfloat16)
    both = lax.all_to_all(
        packed.reshape(experts, capacity, 2 * shard_width),
        "ctx",
        split_axis=0,
        concat_axis=0,
        tiled=True,
    )
    slot_count = both.shape[0] * both.shape[1]
    half = slot_count // 2
    swapped = lax.axis_index("head") % 2 == 1

    def local_order(rows):
        turned = jnp.concatenate([rows[half:], rows[:half]], axis=0)
        return jnp.where(swapped, turned, rows)

    both = local_order(both.reshape(slot_count, 2 * shard_width))
    x_rows = both[:, :shard_width]
    cot_rows = both[:, shard_width:]
    gate_w = w_gate[0]
    up_w = w_up[0]
    down_w = w_down[0]
    gate_part = contract_last(x_rows, gate_w).astype(jnp.bfloat16)
    up_part = contract_last(x_rows, up_w).astype(jnp.bfloat16)
    back_part = contract_last(cot_rows, down_w).astype(jnp.bfloat16)
    head_count = lax.axis_size("head")
    partner = [(i, i ^ 1) for i in range(head_count)]
    same_core = [list(range(c, head_count, 2)) for c in range(2)]
    parts = jnp.stack([gate_part, up_part, back_part])
    pair_sum = (
        parts[:, :half].astype(jnp.float32)
        + lax.ppermute(parts[:, half:], "head", partner).astype(jnp.float32)
    ).astype(jnp.bfloat16)
    pair_sum, chosen_part = lax.optimization_barrier((pair_sum, chosen_part))
    mine = lax.psum(pair_sum, "head", axis_index_groups=same_core)
    chosen = head_sum(chosen_part)
    prob_pairs = jnp.stack(
        [jax.nn.sigmoid(chosen[:, 0] - chosen[:, 1]), jax.nn.sigmoid(chosen[:, 1] - chosen[:, 0])],
        axis=1,
    )
    pair_prod = prob_pairs[:, 0] * prob_pairs[:, 1]
    q_hi = pair_prod.astype(jnp.bfloat16).astype(jnp.float32)
    q_lo = pair_prod - q_hi
    pick_values = jnp.stack(
        [
            prob_pairs.reshape(-1),
            jnp.repeat(q_hi, pick_count),
            jnp.repeat(q_lo, pick_count),
            expert_ids[:, ::-1].reshape(-1).astype(jnp.float32),
        ],
        axis=0,
    )
    slot_values = jnp.sum(
        jnp.where(pick_hit[None], pick_values[:, None, :], 0.0), axis=2
    ).astype(jnp.bfloat16)
    recv_p = lax.all_to_all(
        slot_values.reshape(4, experts, capacity).transpose(1, 0, 2),
        "ctx",
        split_axis=0,
        concat_axis=0,
        tiled=True,
    )
    row_values = local_order(
        recv_p.transpose(0, 2, 1).reshape(slot_count, 4)
    ).T.astype(jnp.float32)
    mine, row_values = lax.optimization_barrier((mine, row_values))
    sums = jnp.concatenate([mine, lax.ppermute(mine, "head", partner)], axis=1)
    gate_sum, up_sum, back_sum = sums[0], sums[1], sums[2]
    prob_rows = row_values[0]
    pair_rows = row_values[1] + row_values[2]
    other_rows = row_values[3].astype(jnp.int32)
    gate_pre = gate_sum.astype(jnp.float32)
    up_pre = up_sum.astype(jnp.float32)
    hidden = forward_act(gate_pre, up_pre)
    back_proj = back_sum.astype(jnp.float32)
    gate_grad, up_grad = backward_act(gate_pre, up_pre, back_proj, prob_rows)
    out_rows = jnp.dot(hidden, down_w, preferred_element_type=jnp.float32).astype(jnp.bfloat16)
    dx_rows = (
        jnp.dot(gate_grad, gate_w, preferred_element_type=jnp.float32)
        + jnp.dot(up_grad, up_w, preferred_element_type=jnp.float32)
    ).astype(jnp.bfloat16)
    hidden_kept = lax.optimization_barrier(hidden)
    scaled = (prob_rows[:, None] * hidden_kept.astype(jnp.float32)).astype(jnp.bfloat16)
    grad_down = contract_rows(scaled, cot_rows).astype(jnp.bfloat16)[None]
    grad_gate = contract_rows(gate_grad, x_rows).astype(jnp.bfloat16)[None]
    grad_up = contract_rows(up_grad, x_rows).astype(jnp.bfloat16)[None]
    score_rows = jnp.sum(hidden.astype(jnp.float32) * back_proj, axis=1)
    own = lax.axis_index("ctx")
    expert_ids_row = jnp.arange(experts, dtype=jnp.int32)[None, :]
    direction = (expert_ids_row == own).astype(jnp.float32) - (
        expert_ids_row == other_rows[:, None]
    ).astype(jnp.float32)
    router_weight = (pair_rows * score_rows)[:, None] * direction
    router_part = jnp.dot(
        x_rows.astype(jnp.float32).T, router_weight, precision=lax.Precision.HIGHEST
    )
    s_hi = score_rows.astype(jnp.bfloat16)
    s_lo = (score_rows - s_hi.astype(jnp.float32)).astype(jnp.bfloat16)
    extra = jnp.zeros((slot_count, 128), jnp.bfloat16).at[:, 0].set(s_hi).at[:, 1].set(s_lo)
    back_both = lax.all_to_all(
        local_order(jnp.concatenate([out_rows, dx_rows, extra], axis=1)).reshape(
            ctx_count, capacity, 2 * shard_width + 128
        ),
        "ctx",
        split_axis=0,
        concat_axis=0,
        tiled=True,
    )
    grad_router = ctx_sum(router_part)
    both_pairs = lax.dot_general(
        pick_hit.astype(jnp.bfloat16),
        back_both.reshape(experts * capacity, 2 * shard_width + 128),
        (((0,), (0,)), ((), ())),
        preferred_element_type=jnp.float32,
    ).reshape(tok_rows, pick_count, 2 * shard_width + 128)
    out_pairs = both_pairs[:, :, :shard_width].astype(jnp.bfloat16)
    dx_pairs = both_pairs[:, :, shard_width : 2 * shard_width].astype(jnp.bfloat16)
    score_grad = both_pairs[:, :, 2 * shard_width] + both_pairs[:, :, 2 * shard_width + 1]
    mixed = jnp.sum(prob_pairs[:, :, None] * out_pairs.astype(jnp.float32), axis=1).astype(
        jnp.bfloat16
    )
    logit_lead = prob_pairs[:, 0] * prob_pairs[:, 1] * (score_grad[:, 0] - score_grad[:, 1])
    logit_grad = jnp.stack([logit_lead, -logit_lead], axis=1)
    dense_grad = jnp.sum(logit_grad[:, :, None] * onehot, axis=1)
    router_term = jnp.dot(
        dense_grad, w_router.astype(jnp.float32).T, precision=lax.Precision.HIGHEST
    )
    grad_tokens = (
        dx_pairs[:, 0].astype(jnp.float32) + dx_pairs[:, 1].astype(jnp.float32) + router_term
    ).astype(jnp.bfloat16)
    return (mixed, grad_tokens, grad_router, grad_gate, grad_up, grad_down)


def solution(mesh):
    placed = (
        P("ctx", "head"),
        P("ctx", "head"),
        P("ctx", None),
        P("head", None),
        P("ctx", None, "head"),
        P("ctx", None, "head"),
        P("ctx", None, "head"),
    )
    return jax.shard_map(
        local,
        mesh=mesh,
        in_specs=placed,
        out_specs=(
            P("ctx", "head"),
            P("ctx", "head"),
            P("head", None),
            P("ctx", None, "head"),
            P("ctx", None, "head"),
            P("ctx", None, "head"),
        ),
        check_vma=False,
    )
```

```python
import jax
import jax.numpy as jnp
from jax import lax
from jax.sharding import PartitionSpec as P


def contract_rows(left, right):
    return lax.dot_general(
        left, right, (((0,), (0,)), ((), ())), preferred_element_type=jnp.float32
    )


def contract_last(left, right):
    return lax.dot_general(
        left, right, (((1,), (1,)), ((), ())), preferred_element_type=jnp.float32
    )


def forward_act(gate_pre, up_pre):
    sigma = jax.nn.sigmoid(gate_pre)
    active = gate_pre * sigma
    return (active * up_pre).astype(jnp.bfloat16)


def backward_act(gate_pre, up_pre, back_proj, prob_rows):
    sigma = jax.nn.sigmoid(gate_pre)
    active = gate_pre * sigma
    hidden_grad = prob_rows[:, None] * back_proj
    gate_grad = (hidden_grad * up_pre * sigma * (1.0 + gate_pre * (1.0 - sigma))).astype(
        jnp.bfloat16
    )
    up_grad = (hidden_grad * active).astype(jnp.bfloat16)
    return (gate_grad, up_grad)


def head_sum(part):
    count = lax.axis_size("head")
    spread = jnp.broadcast_to(part[None], (count,) + part.shape)
    gathered = lax.all_to_all(spread, "head", split_axis=0, concat_axis=0, tiled=True)
    return jnp.sum(gathered, axis=0)


def ctx_sum(part):
    count = lax.axis_size("ctx")
    rows = part.shape[0]
    pieces = part.reshape(count, rows // count, part.shape[1])
    mine = jnp.sum(lax.all_to_all(pieces, "ctx", split_axis=0, concat_axis=0, tiled=True), axis=0)
    spread = jnp.broadcast_to(mine[None], pieces.shape)
    return lax.all_to_all(spread, "ctx", split_axis=0, concat_axis=0, tiled=True).reshape(part.shape)


def local(tokens, cotangent, expert_ids, w_router, w_gate, w_up, w_down):
    ctx_count = lax.axis_size("ctx")
    tok_rows = tokens.shape[0]
    shard_width = tokens.shape[1]
    pick_count = expert_ids.shape[1]
    experts = w_router.shape[1]
    capacity = 3 * tok_rows * pick_count // (2 * experts)
    partial_logits = jnp.dot(tokens, w_router, preferred_element_type=jnp.float32)
    onehot = (expert_ids[:, :, None] == jnp.arange(experts, dtype=jnp.int32)[None, None, :]).astype(
        jnp.float32
    )
    chosen_part = jnp.sum(partial_logits[:, None, :] * onehot, axis=2)
    flat_ids = expert_ids.reshape(-1)
    id_hits = (flat_ids[:, None] == jnp.arange(experts, dtype=jnp.int32)[None, :]).astype(jnp.int32)
    places = jnp.sum((jnp.cumsum(id_hits, axis=0) - 1) * id_hits, axis=1)
    slot_index = flat_ids * capacity + places
    slot_ids = jnp.arange(experts * capacity, dtype=jnp.int32)
    pick_hit = slot_ids[:, None] == slot_index[None, :]
    token_hit = pick_hit.reshape(experts * capacity, tok_rows, pick_count).any(axis=2)
    rows_in = jnp.concatenate([tokens, cotangent], axis=1)
    packed = jnp.dot(
        token_hit.astype(jnp.bfloat16), rows_in, preferred_element_type=jnp.float32
    ).astype(jnp.bfloat16)
    both = lax.all_to_all(
        packed.reshape(experts, capacity, 2 * shard_width),
        "ctx",
        split_axis=0,
        concat_axis=0,
        tiled=True,
    )
    slot_count = both.shape[0] * both.shape[1]
    half = slot_count // 2
    swapped = lax.axis_index("head") % 2 == 1

    def local_order(rows):
        turned = jnp.concatenate([rows[half:], rows[:half]], axis=0)
        return jnp.where(swapped, turned, rows)

    both = local_order(both.reshape(slot_count, 2 * shard_width))
    x_rows = both[:, :shard_width]
    cot_rows = both[:, shard_width:]
    gate_w = w_gate[0]
    up_w = w_up[0]
    down_w = w_down[0]
    gate_part = contract_last(x_rows, gate_w).astype(jnp.bfloat16)
    up_part = contract_last(x_rows, up_w).astype(jnp.bfloat16)
    back_part = contract_last(cot_rows, down_w).astype(jnp.bfloat16)
    head_count = lax.axis_size("head")
    partner = [(i, i ^ 1) for i in range(head_count)]
    same_core = [list(range(c, head_count, 2)) for c in range(2)]
    parts = jnp.stack([gate_part, up_part, back_part])
    pair_sum = (
        parts[:, :half].astype(jnp.float32)
        + lax.ppermute(parts[:, half:], "head", partner).astype(jnp.float32)
    ).astype(jnp.bfloat16)
    pair_sum, chosen_part = lax.optimization_barrier((pair_sum, chosen_part))
    mine = lax.psum(pair_sum, "head", axis_index_groups=same_core)
    chosen = head_sum(chosen_part)
    prob_pairs = jnp.stack(
        [jax.nn.sigmoid(chosen[:, 0] - chosen[:, 1]), jax.nn.sigmoid(chosen[:, 1] - chosen[:, 0])],
        axis=1,
    )
    pair_prod = prob_pairs[:, 0] * prob_pairs[:, 1]
    q_hi = pair_prod.astype(jnp.bfloat16).astype(jnp.float32)
    q_lo = pair_prod - q_hi
    pick_values = jnp.stack(
        [
            prob_pairs.reshape(-1),
            jnp.repeat(q_hi, pick_count),
            jnp.repeat(q_lo, pick_count),
            expert_ids[:, ::-1].reshape(-1).astype(jnp.float32),
        ],
        axis=0,
    )
    slot_values = jnp.sum(
        jnp.where(pick_hit[None], pick_values[:, None, :], 0.0), axis=2
    ).astype(jnp.bfloat16)
    recv_p = lax.all_to_all(
        slot_values.reshape(4, experts, capacity).transpose(1, 0, 2),
        "ctx",
        split_axis=0,
        concat_axis=0,
        tiled=True,
    )
    row_values = local_order(
        recv_p.transpose(0, 2, 1).reshape(slot_count, 4)
    ).T.astype(jnp.float32)
    mine, row_values = lax.optimization_barrier((mine, row_values))
    sums = jnp.concatenate([mine, lax.ppermute(mine, "head", partner)], axis=1)
    gate_sum, up_sum, back_sum = sums[0], sums[1], sums[2]
    prob_rows = row_values[0]
    pair_rows = row_values[1] + row_values[2]
    other_rows = row_values[3].astype(jnp.int32)
    gate_pre = gate_sum.astype(jnp.float32)
    up_pre = up_sum.astype(jnp.float32)
    hidden = forward_act(gate_pre, up_pre)
    back_proj = back_sum.astype(jnp.float32)
    gate_grad, up_grad = backward_act(gate_pre, up_pre, back_proj, prob_rows)
    out_rows = jnp.dot(hidden, down_w, preferred_element_type=jnp.float32).astype(jnp.bfloat16)
    dx_rows = (
        jnp.dot(gate_grad, gate_w, preferred_element_type=jnp.float32)
        + jnp.dot(up_grad, up_w, preferred_element_type=jnp.float32)
    ).astype(jnp.bfloat16)
    hidden_kept = lax.optimization_barrier(hidden)
    scaled = (prob_rows[:, None] * hidden_kept.astype(jnp.float32)).astype(jnp.bfloat16)
    grad_down = contract_rows(scaled, cot_rows).astype(jnp.bfloat16)[None]
    grad_gate = contract_rows(gate_grad, x_rows).astype(jnp.bfloat16)[None]
    grad_up = contract_rows(up_grad, x_rows).astype(jnp.bfloat16)[None]
    score_rows = jnp.sum(hidden.astype(jnp.float32) * back_proj, axis=1)
    own = lax.axis_index("ctx")
    expert_ids_row = jnp.arange(experts, dtype=jnp.int32)[None, :]
    direction = (expert_ids_row == own).astype(jnp.float32) - (
        expert_ids_row == other_rows[:, None]
    ).astype(jnp.float32)
    router_weight = (pair_rows * score_rows)[:, None] * direction
    router_part = jnp.dot(
        x_rows.astype(jnp.float32).T, router_weight, precision=lax.Precision.HIGHEST
    )
    s_hi = score_rows.astype(jnp.bfloat16)
    s_lo = (score_rows - s_hi.astype(jnp.float32)).astype(jnp.bfloat16)
    extra = jnp.zeros((slot_count, 128), jnp.bfloat16).at[:, 0].set(s_hi).at[:, 1].set(s_lo)
    back_both = lax.all_to_all(
        local_order(jnp.concatenate([out_rows, dx_rows, extra], axis=1)).reshape(
            ctx_count, capacity, 2 * shard_width + 128
        ),
        "ctx",
        split_axis=0,
        concat_axis=0,
        tiled=True,
    )
    router_part, back_both = lax.optimization_barrier((router_part, back_both))
    grad_router = ctx_sum(router_part)
    both_pairs = lax.dot_general(
        pick_hit.astype(jnp.bfloat16),
        back_both.reshape(experts * capacity, 2 * shard_width + 128),
        (((0,), (0,)), ((), ())),
        preferred_element_type=jnp.float32,
    ).reshape(tok_rows, pick_count, 2 * shard_width + 128)
    out_pairs = both_pairs[:, :, :shard_width].astype(jnp.bfloat16)
    dx_pairs = both_pairs[:, :, shard_width : 2 * shard_width].astype(jnp.bfloat16)
    score_grad = both_pairs[:, :, 2 * shard_width] + both_pairs[:, :, 2 * shard_width + 1]
    mixed = jnp.sum(prob_pairs[:, :, None] * out_pairs.astype(jnp.float32), axis=1).astype(
        jnp.bfloat16
    )
    logit_lead = prob_pairs[:, 0] * prob_pairs[:, 1] * (score_grad[:, 0] - score_grad[:, 1])
    logit_grad = jnp.stack([logit_lead, -logit_lead], axis=1)
    dense_grad = jnp.sum(logit_grad[:, :, None] * onehot, axis=1)
    router_term = jnp.dot(
        dense_grad, w_router.astype(jnp.float32).T, precision=lax.Precision.HIGHEST
    )
    grad_tokens = (
        dx_pairs[:, 0].astype(jnp.float32) + dx_pairs[:, 1].astype(jnp.float32) + router_term
    ).astype(jnp.bfloat16)
    return (mixed, grad_tokens, grad_router, grad_gate, grad_up, grad_down)


def solution(mesh):
    placed = (
        P("ctx", "head"),
        P("ctx", "head"),
        P("ctx", None),
        P("head", None),
        P("ctx", None, "head"),
        P("ctx", None, "head"),
        P("ctx", None, "head"),
    )
    return jax.shard_map(
        local,
        mesh=mesh,
        in_specs=placed,
        out_specs=(
            P("ctx", "head"),
            P("ctx", "head"),
            P("head", None),
            P("ctx", None, "head"),
            P("ctx", None, "head"),
            P("ctx", None, "head"),
        ),
        check_vma=False,
    )
```

```python
import jax
import jax.numpy as jnp
from jax import lax
from jax.sharding import PartitionSpec as P


def contract_rows(left, right):
    return lax.dot_general(
        left, right, (((0,), (0,)), ((), ())), preferred_element_type=jnp.float32
    )


def contract_last(left, right):
    return lax.dot_general(
        left, right, (((1,), (1,)), ((), ())), preferred_element_type=jnp.float32
    )


def forward_act(gate_pre, up_pre):
    sigma = jax.nn.sigmoid(gate_pre)
    active = gate_pre * sigma
    return (active * up_pre).astype(jnp.bfloat16)


def backward_act(gate_pre, up_pre, back_proj, prob_rows):
    sigma = jax.nn.sigmoid(gate_pre)
    active = gate_pre * sigma
    hidden_grad = prob_rows[:, None] * back_proj
    gate_grad = (hidden_grad * up_pre * sigma * (1.0 + gate_pre * (1.0 - sigma))).astype(
        jnp.bfloat16
    )
    up_grad = (hidden_grad * active).astype(jnp.bfloat16)
    return (gate_grad, up_grad)


def head_sum(part):
    count = lax.axis_size("head")
    spread = jnp.broadcast_to(part[None], (count,) + part.shape)
    gathered = lax.all_to_all(spread, "head", split_axis=0, concat_axis=0, tiled=True)
    return jnp.sum(gathered, axis=0)


def ctx_sum(part):
    count = lax.axis_size("ctx")
    rows = part.shape[0]
    pieces = part.reshape(count, rows // count, part.shape[1])
    mine = jnp.sum(lax.all_to_all(pieces, "ctx", split_axis=0, concat_axis=0, tiled=True), axis=0)
    spread = jnp.broadcast_to(mine[None], pieces.shape)
    return lax.all_to_all(spread, "ctx", split_axis=0, concat_axis=0, tiled=True).reshape(part.shape)


def local(tokens, cotangent, expert_ids, w_router, w_gate, w_up, w_down):
    ctx_count = lax.axis_size("ctx")
    tok_rows = tokens.shape[0]
    shard_width = tokens.shape[1]
    pick_count = expert_ids.shape[1]
    experts = w_router.shape[1]
    capacity = 3 * tok_rows * pick_count // (2 * experts)
    partial_logits = jnp.dot(tokens, w_router, preferred_element_type=jnp.float32)
    onehot = (expert_ids[:, :, None] == jnp.arange(experts, dtype=jnp.int32)[None, None, :]).astype(
        jnp.float32
    )
    chosen_part = jnp.sum(partial_logits[:, None, :] * onehot, axis=2)
    flat_ids = expert_ids.reshape(-1)
    id_hits = (flat_ids[:, None] == jnp.arange(experts, dtype=jnp.int32)[None, :]).astype(jnp.int32)
    places = jnp.sum((jnp.cumsum(id_hits, axis=0) - 1) * id_hits, axis=1)
    slot_index = flat_ids * capacity + places
    slot_ids = jnp.arange(experts * capacity, dtype=jnp.int32)
    pick_hit = slot_ids[:, None] == slot_index[None, :]
    token_hit = pick_hit.reshape(experts * capacity, tok_rows, pick_count).any(axis=2)
    rows_in = jnp.concatenate([tokens, cotangent], axis=1)
    packed = jnp.dot(
        token_hit.astype(jnp.bfloat16), rows_in, preferred_element_type=jnp.float32
    ).astype(jnp.bfloat16)
    both = lax.all_to_all(
        packed.reshape(experts, capacity, 2 * shard_width),
        "ctx",
        split_axis=0,
        concat_axis=0,
        tiled=True,
    )
    slot_count = both.shape[0] * both.shape[1]
    half = slot_count // 2
    swapped = lax.axis_index("head") % 2 == 1

    def local_order(rows):
        turned = jnp.concatenate([rows[half:], rows[:half]], axis=0)
        return jnp.where(swapped, turned, rows)

    both = local_order(both.reshape(slot_count, 2 * shard_width))
    x_rows = both[:, :shard_width]
    cot_rows = both[:, shard_width:]
    gate_w = w_gate[0]
    up_w = w_up[0]
    down_w = w_down[0]
    gate_part = contract_last(x_rows, gate_w).astype(jnp.bfloat16)
    up_part = contract_last(x_rows, up_w).astype(jnp.bfloat16)
    back_part = contract_last(cot_rows, down_w).astype(jnp.bfloat16)
    head_count = lax.axis_size("head")
    partner = [(i, i ^ 1) for i in range(head_count)]
    same_core = [list(range(c, head_count, 2)) for c in range(2)]
    parts = jnp.stack([gate_part, up_part, back_part])
    pair_sum = (
        parts[:, :half].astype(jnp.float32)
        + lax.ppermute(parts[:, half:], "head", partner).astype(jnp.float32)
    ).astype(jnp.bfloat16)
    pair_sum, chosen_part = lax.optimization_barrier((pair_sum, chosen_part))
    mine = lax.psum(pair_sum, "head", axis_index_groups=same_core)
    chosen = head_sum(chosen_part)
    prob_pairs = jnp.stack(
        [jax.nn.sigmoid(chosen[:, 0] - chosen[:, 1]), jax.nn.sigmoid(chosen[:, 1] - chosen[:, 0])],
        axis=1,
    )
    pair_prod = prob_pairs[:, 0] * prob_pairs[:, 1]
    q_hi = pair_prod.astype(jnp.bfloat16).astype(jnp.float32)
    q_lo = pair_prod - q_hi
    pick_values = jnp.stack(
        [
            prob_pairs.reshape(-1),
            jnp.repeat(q_hi, pick_count),
            jnp.repeat(q_lo, pick_count),
            expert_ids[:, ::-1].reshape(-1).astype(jnp.float32),
        ],
        axis=0,
    )
    slot_values = jnp.sum(
        jnp.where(pick_hit[None], pick_values[:, None, :], 0.0), axis=2
    ).astype(jnp.bfloat16)
    recv_p = lax.all_to_all(
        slot_values.reshape(4, experts, capacity).transpose(1, 0, 2),
        "ctx",
        split_axis=0,
        concat_axis=0,
        tiled=True,
    )
    row_values = local_order(
        recv_p.transpose(0, 2, 1).reshape(slot_count, 4)
    ).T.astype(jnp.float32)
    mine, row_values = lax.optimization_barrier((mine, row_values))
    sums = jnp.concatenate([mine, lax.ppermute(mine, "head", partner)], axis=1)
    gate_sum, up_sum, back_sum = sums[0], sums[1], sums[2]
    prob_rows = row_values[0]
    pair_rows = row_values[1] + row_values[2]
    other_rows = row_values[3].astype(jnp.int32)
    gate_pre = gate_sum.astype(jnp.float32)
    up_pre = up_sum.astype(jnp.float32)
    hidden = forward_act(gate_pre, up_pre)
    back_proj = back_sum.astype(jnp.float32)
    gate_grad, up_grad = backward_act(gate_pre, up_pre, back_proj, prob_rows)
    out_rows = jnp.dot(hidden, down_w, preferred_element_type=jnp.float32).astype(jnp.bfloat16)
    dx_rows = (
        jnp.dot(gate_grad, gate_w, preferred_element_type=jnp.float32)
        + jnp.dot(up_grad, up_w, preferred_element_type=jnp.float32)
    ).astype(jnp.bfloat16)
    hidden_kept = lax.optimization_barrier(hidden)
    scaled = (prob_rows[:, None] * hidden_kept.astype(jnp.float32)).astype(jnp.bfloat16)
    grad_down = contract_rows(scaled, cot_rows).astype(jnp.bfloat16)[None]
    grad_gate = contract_rows(gate_grad, x_rows).astype(jnp.bfloat16)[None]
    grad_up = contract_rows(up_grad, x_rows).astype(jnp.bfloat16)[None]
    score_rows = jnp.sum(hidden.astype(jnp.float32) * back_proj, axis=1)
    own = lax.axis_index("ctx")
    expert_ids_row = jnp.arange(experts, dtype=jnp.int32)[None, :]
    direction = (expert_ids_row == own).astype(jnp.float32) - (
        expert_ids_row == other_rows[:, None]
    ).astype(jnp.float32)
    router_weight = (pair_rows * score_rows)[:, None] * direction
    router_part = jnp.dot(
        x_rows.astype(jnp.float32).T, router_weight, precision=lax.Precision.HIGHEST
    )
    s_hi = score_rows.astype(jnp.bfloat16)
    s_lo = (score_rows - s_hi.astype(jnp.float32)).astype(jnp.bfloat16)
    extra = jnp.zeros((slot_count, 128), jnp.bfloat16).at[:, 0].set(s_hi).at[:, 1].set(s_lo)
    router_pieces = router_part.reshape(ctx_count, -1)
    router_hi = router_pieces.astype(jnp.bfloat16)
    router_lo = (router_pieces - router_hi.astype(jnp.float32)).astype(jnp.bfloat16)
    router_row = jnp.concatenate([router_hi, router_lo], axis=1)
    row_width = 2 * shard_width + 128
    router_row = jnp.pad(router_row, ((0, 0), (0, row_width - router_row.shape[1])))
    payload = jnp.concatenate(
        [
            local_order(jnp.concatenate([out_rows, dx_rows, extra], axis=1)).reshape(
                ctx_count, capacity, row_width
            ),
            router_row[:, None, :],
        ],
        axis=1,
    )
    back_both = lax.all_to_all(payload, "ctx", split_axis=0, concat_axis=0, tiled=True)
    piece = router_pieces.shape[1]
    router_in = back_both[:, capacity, : 2 * piece].astype(jnp.float32)
    router_mine = jnp.sum(router_in[:, :piece] + router_in[:, piece:], axis=0)
    grad_router = lax.all_to_all(
        jnp.broadcast_to(router_mine[None], router_pieces.shape),
        "ctx",
        split_axis=0,
        concat_axis=0,
        tiled=True,
    ).reshape(router_part.shape)
    both_pairs = lax.dot_general(
        pick_hit.astype(jnp.bfloat16),
        back_both[:, :capacity].reshape(experts * capacity, row_width),
        (((0,), (0,)), ((), ())),
        preferred_element_type=jnp.float32,
    ).reshape(tok_rows, pick_count, row_width)
    out_pairs = both_pairs[:, :, :shard_width].astype(jnp.bfloat16)
    dx_pairs = both_pairs[:, :, shard_width : 2 * shard_width].astype(jnp.bfloat16)
    score_grad = both_pairs[:, :, 2 * shard_width] + both_pairs[:, :, 2 * shard_width + 1]
    mixed = jnp.sum(prob_pairs[:, :, None] * out_pairs.astype(jnp.float32), axis=1).astype(
        jnp.bfloat16
    )
    logit_lead = prob_pairs[:, 0] * prob_pairs[:, 1] * (score_grad[:, 0] - score_grad[:, 1])
    logit_grad = jnp.stack([logit_lead, -logit_lead], axis=1)
    dense_grad = jnp.sum(logit_grad[:, :, None] * onehot, axis=1)
    router_term = jnp.dot(
        dense_grad, w_router.astype(jnp.float32).T, precision=lax.Precision.HIGHEST
    )
    grad_tokens = (
        dx_pairs[:, 0].astype(jnp.float32) + dx_pairs[:, 1].astype(jnp.float32) + router_term
    ).astype(jnp.bfloat16)
    return (mixed, grad_tokens, grad_router, grad_gate, grad_up, grad_down)


def solution(mesh):
    placed = (
        P("ctx", "head"),
        P("ctx", "head"),
        P("ctx", None),
        P("head", None),
        P("ctx", None, "head"),
        P("ctx", None, "head"),
        P("ctx", None, "head"),
    )
    return jax.shard_map(
        local,
        mesh=mesh,
        in_specs=placed,
        out_specs=(
            P("ctx", "head"),
            P("ctx", "head"),
            P("head", None),
            P("ctx", None, "head"),
            P("ctx", None, "head"),
            P("ctx", None, "head"),
        ),
        check_vma=False,
    )
```

```python
import jax
import jax.numpy as jnp
from jax import lax
from jax.sharding import PartitionSpec as P


def contract_rows(left, right):
    return lax.dot_general(
        left, right, (((0,), (0,)), ((), ())), preferred_element_type=jnp.float32
    )


def contract_last(left, right):
    return lax.dot_general(
        left, right, (((1,), (1,)), ((), ())), preferred_element_type=jnp.float32
    )


def forward_act(gate_pre, up_pre):
    sigma = jax.nn.sigmoid(gate_pre)
    active = gate_pre * sigma
    return (active * up_pre).astype(jnp.bfloat16)


def backward_act(gate_pre, up_pre, back_proj, prob_rows):
    sigma = jax.nn.sigmoid(gate_pre)
    active = gate_pre * sigma
    hidden_grad = prob_rows[:, None] * back_proj
    gate_grad = (hidden_grad * up_pre * sigma * (1.0 + gate_pre * (1.0 - sigma))).astype(
        jnp.bfloat16
    )
    up_grad = (hidden_grad * active).astype(jnp.bfloat16)
    return (gate_grad, up_grad)


def head_sum(part):
    count = lax.axis_size("head")
    spread = jnp.broadcast_to(part[None], (count,) + part.shape)
    gathered = lax.all_to_all(spread, "head", split_axis=0, concat_axis=0, tiled=True)
    return jnp.sum(gathered, axis=0)


def ctx_sum(part):
    count = lax.axis_size("ctx")
    rows = part.shape[0]
    pieces = part.reshape(count, rows // count, part.shape[1])
    mine = jnp.sum(lax.all_to_all(pieces, "ctx", split_axis=0, concat_axis=0, tiled=True), axis=0)
    spread = jnp.broadcast_to(mine[None], pieces.shape)
    return lax.all_to_all(spread, "ctx", split_axis=0, concat_axis=0, tiled=True).reshape(part.shape)


def local(tokens, cotangent, expert_ids, w_router, w_gate, w_up, w_down):
    ctx_count = lax.axis_size("ctx")
    tok_rows = tokens.shape[0]
    shard_width = tokens.shape[1]
    pick_count = expert_ids.shape[1]
    experts = w_router.shape[1]
    capacity = 3 * tok_rows * pick_count // (2 * experts)
    partial_logits = jnp.dot(tokens, w_router, preferred_element_type=jnp.float32)
    onehot = (expert_ids[:, :, None] == jnp.arange(experts, dtype=jnp.int32)[None, None, :]).astype(
        jnp.float32
    )
    chosen_part = jnp.sum(partial_logits[:, None, :] * onehot, axis=2)
    flat_ids = expert_ids.reshape(-1)
    id_hits = (flat_ids[:, None] == jnp.arange(experts, dtype=jnp.int32)[None, :]).astype(jnp.int32)
    places = jnp.sum((jnp.cumsum(id_hits, axis=0) - 1) * id_hits, axis=1)
    slot_index = flat_ids * capacity + places
    slot_ids = jnp.arange(experts * capacity, dtype=jnp.int32)
    pick_hit = slot_ids[:, None] == slot_index[None, :]
    token_hit = pick_hit.reshape(experts * capacity, tok_rows, pick_count).any(axis=2)
    rows_in = jnp.concatenate([tokens, cotangent], axis=1)
    packed = jnp.dot(
        token_hit.astype(jnp.bfloat16), rows_in, preferred_element_type=jnp.float32
    ).astype(jnp.bfloat16)
    both = lax.all_to_all(
        packed.reshape(experts, capacity, 2 * shard_width),
        "ctx",
        split_axis=0,
        concat_axis=0,
        tiled=True,
    )
    slot_count = both.shape[0] * both.shape[1]
    half = slot_count // 2
    swapped = lax.axis_index("head") % 2 == 1

    def local_order(rows):
        turned = jnp.concatenate([rows[half:], rows[:half]], axis=0)
        return jnp.where(swapped, turned, rows)

    both = local_order(both.reshape(slot_count, 2 * shard_width))
    x_rows = both[:, :shard_width]
    cot_rows = both[:, shard_width:]
    gate_w = w_gate[0]
    up_w = w_up[0]
    down_w = w_down[0]
    gate_part = contract_last(x_rows, gate_w).astype(jnp.bfloat16)
    up_part = contract_last(x_rows, up_w).astype(jnp.bfloat16)
    back_part = contract_last(cot_rows, down_w).astype(jnp.bfloat16)
    head_count = lax.axis_size("head")
    partner = [(i, i ^ 1) for i in range(head_count)]
    same_core = [list(range(c, head_count, 2)) for c in range(2)]
    parts = jnp.stack([gate_part, up_part, back_part])
    pair_sum = (
        parts[:, :half].astype(jnp.float32)
        + lax.ppermute(parts[:, half:], "head", partner).astype(jnp.float32)
    ).astype(jnp.bfloat16)
    pair_sum, chosen_part = lax.optimization_barrier((pair_sum, chosen_part))
    mine = lax.psum(pair_sum, "head", axis_index_groups=same_core)
    chosen = head_sum(chosen_part)
    prob_pairs = jnp.stack(
        [jax.nn.sigmoid(chosen[:, 0] - chosen[:, 1]), jax.nn.sigmoid(chosen[:, 1] - chosen[:, 0])],
        axis=1,
    )
    pair_prod = prob_pairs[:, 0] * prob_pairs[:, 1]
    q_hi = pair_prod.astype(jnp.bfloat16).astype(jnp.float32)
    q_lo = pair_prod - q_hi
    pick_values = jnp.stack(
        [
            prob_pairs.reshape(-1),
            jnp.repeat(q_hi, pick_count),
            jnp.repeat(q_lo, pick_count),
            expert_ids[:, ::-1].reshape(-1).astype(jnp.float32),
        ],
        axis=0,
    )
    slot_values = jnp.sum(
        jnp.where(pick_hit[None], pick_values[:, None, :], 0.0), axis=2
    ).astype(jnp.bfloat16)
    recv_p = lax.all_to_all(
        slot_values.reshape(4, experts, capacity).transpose(1, 0, 2),
        "ctx",
        split_axis=0,
        concat_axis=0,
        tiled=True,
    )
    row_values = local_order(
        recv_p.transpose(0, 2, 1).reshape(slot_count, 4)
    ).T.astype(jnp.float32)
    mine, row_values = lax.optimization_barrier((mine, row_values))
    sums = jnp.concatenate([mine, lax.ppermute(mine, "head", partner)], axis=1)
    gate_sum, up_sum, back_sum = sums[0], sums[1], sums[2]
    prob_rows = row_values[0]
    pair_rows = row_values[1] + row_values[2]
    other_rows = row_values[3].astype(jnp.int32)
    gate_pre = gate_sum.astype(jnp.float32)
    up_pre = up_sum.astype(jnp.float32)
    hidden = forward_act(gate_pre, up_pre)
    back_proj = back_sum.astype(jnp.float32)
    gate_grad, up_grad = backward_act(gate_pre, up_pre, back_proj, prob_rows)
    out_rows = jnp.dot(hidden, down_w, preferred_element_type=jnp.float32).astype(jnp.bfloat16)
    dx_rows = (
        jnp.dot(gate_grad, gate_w, preferred_element_type=jnp.float32)
        + jnp.dot(up_grad, up_w, preferred_element_type=jnp.float32)
    ).astype(jnp.bfloat16)
    hidden_kept = lax.optimization_barrier(hidden)
    scaled = (prob_rows[:, None] * hidden_kept.astype(jnp.float32)).astype(jnp.bfloat16)
    grad_down = contract_rows(scaled, cot_rows).astype(jnp.bfloat16)[None]
    grad_gate = contract_rows(gate_grad, x_rows).astype(jnp.bfloat16)[None]
    grad_up = contract_rows(up_grad, x_rows).astype(jnp.bfloat16)[None]
    score_rows = jnp.sum(hidden.astype(jnp.float32) * back_proj, axis=1)
    own = lax.axis_index("ctx")
    expert_ids_row = jnp.arange(experts, dtype=jnp.int32)[None, :]
    direction = (expert_ids_row == own).astype(jnp.float32) - (
        expert_ids_row == other_rows[:, None]
    ).astype(jnp.float32)
    router_weight = (pair_rows * score_rows)[:, None] * direction
    router_part = jnp.dot(
        x_rows.astype(jnp.float32).T, router_weight, precision=lax.Precision.HIGHEST
    )
    s_hi = score_rows.astype(jnp.bfloat16)
    s_lo = (score_rows - s_hi.astype(jnp.float32)).astype(jnp.bfloat16)
    router_pieces = router_part.reshape(ctx_count, -1)
    router_hi = router_pieces.astype(jnp.bfloat16)
    router_lo = (router_pieces - router_hi.astype(jnp.float32)).astype(jnp.bfloat16)
    spare = 126
    router_cols = jnp.concatenate([router_hi, router_lo], axis=1)
    router_cols = jnp.pad(
        router_cols, ((0, 0), (0, capacity * spare - router_cols.shape[1]))
    ).reshape(ctx_count, capacity, spare)
    row_width = 2 * shard_width + 128
    main = local_order(
        jnp.concatenate([out_rows, dx_rows, s_hi[:, None], s_lo[:, None]], axis=1)
    ).reshape(ctx_count, capacity, row_width - spare)
    payload = jnp.concatenate([main, router_cols], axis=2)
    back_both = lax.all_to_all(payload, "ctx", split_axis=0, concat_axis=0, tiled=True)
    piece = router_pieces.shape[1]
    router_in = (
        back_both[:, :, row_width - spare :]
        .reshape(ctx_count, capacity * spare)[:, : 2 * piece]
        .astype(jnp.float32)
    )
    router_mine = jnp.sum(router_in[:, :piece] + router_in[:, piece:], axis=0)
    grad_router = lax.all_to_all(
        jnp.broadcast_to(router_mine[None], router_pieces.shape),
        "ctx",
        split_axis=0,
        concat_axis=0,
        tiled=True,
    ).reshape(router_part.shape)
    both_pairs = lax.dot_general(
        pick_hit.astype(jnp.bfloat16),
        back_both.reshape(experts * capacity, row_width),
        (((0,), (0,)), ((), ())),
        preferred_element_type=jnp.float32,
    ).reshape(tok_rows, pick_count, row_width)
    out_pairs = both_pairs[:, :, :shard_width].astype(jnp.bfloat16)
    dx_pairs = both_pairs[:, :, shard_width : 2 * shard_width].astype(jnp.bfloat16)
    score_grad = both_pairs[:, :, 2 * shard_width] + both_pairs[:, :, 2 * shard_width + 1]
    mixed = jnp.sum(prob_pairs[:, :, None] * out_pairs.astype(jnp.float32), axis=1).astype(
        jnp.bfloat16
    )
    logit_lead = prob_pairs[:, 0] * prob_pairs[:, 1] * (score_grad[:, 0] - score_grad[:, 1])
    logit_grad = jnp.stack([logit_lead, -logit_lead], axis=1)
    dense_grad = jnp.sum(logit_grad[:, :, None] * onehot, axis=1)
    router_term = jnp.dot(
        dense_grad, w_router.astype(jnp.float32).T, precision=lax.Precision.HIGHEST
    )
    grad_tokens = (
        dx_pairs[:, 0].astype(jnp.float32) + dx_pairs[:, 1].astype(jnp.float32) + router_term
    ).astype(jnp.bfloat16)
    return (mixed, grad_tokens, grad_router, grad_gate, grad_up, grad_down)


def solution(mesh):
    placed = (
        P("ctx", "head"),
        P("ctx", "head"),
        P("ctx", None),
        P("head", None),
        P("ctx", None, "head"),
        P("ctx", None, "head"),
        P("ctx", None, "head"),
    )
    return jax.shard_map(
        local,
        mesh=mesh,
        in_specs=placed,
        out_specs=(
            P("ctx", "head"),
            P("ctx", "head"),
            P("head", None),
            P("ctx", None, "head"),
            P("ctx", None, "head"),
            P("ctx", None, "head"),
        ),
        check_vma=False,
    )
```

```python
import jax
import jax.numpy as jnp
from jax import lax
from jax.sharding import PartitionSpec as P


def contract_rows(left, right):
    return lax.dot_general(
        left, right, (((0,), (0,)), ((), ())), preferred_element_type=jnp.float32
    )


def contract_last(left, right):
    return lax.dot_general(
        left, right, (((1,), (1,)), ((), ())), preferred_element_type=jnp.float32
    )


def forward_act(gate_pre, up_pre):
    sigma = jax.nn.sigmoid(gate_pre)
    active = gate_pre * sigma
    return (active * up_pre).astype(jnp.bfloat16)


def backward_act(gate_pre, up_pre, back_proj, prob_rows):
    sigma = jax.nn.sigmoid(gate_pre)
    active = gate_pre * sigma
    hidden_grad = prob_rows[:, None] * back_proj
    gate_grad = (hidden_grad * up_pre * sigma * (1.0 + gate_pre * (1.0 - sigma))).astype(
        jnp.bfloat16
    )
    up_grad = (hidden_grad * active).astype(jnp.bfloat16)
    return (gate_grad, up_grad)


def head_sum(part):
    count = lax.axis_size("head")
    spread = jnp.broadcast_to(part[None], (count,) + part.shape)
    gathered = lax.all_to_all(spread, "head", split_axis=0, concat_axis=0, tiled=True)
    return jnp.sum(gathered, axis=0)


def ctx_sum(part):
    count = lax.axis_size("ctx")
    rows = part.shape[0]
    pieces = part.reshape(count, rows // count, part.shape[1])
    mine = jnp.sum(lax.all_to_all(pieces, "ctx", split_axis=0, concat_axis=0, tiled=True), axis=0)
    spread = jnp.broadcast_to(mine[None], pieces.shape)
    return lax.all_to_all(spread, "ctx", split_axis=0, concat_axis=0, tiled=True).reshape(part.shape)


def local(tokens, cotangent, expert_ids, w_router, w_gate, w_up, w_down):
    ctx_count = lax.axis_size("ctx")
    tok_rows = tokens.shape[0]
    shard_width = tokens.shape[1]
    pick_count = expert_ids.shape[1]
    experts = w_router.shape[1]
    capacity = 3 * tok_rows * pick_count // (2 * experts)
    partial_logits = jnp.dot(tokens, w_router, preferred_element_type=jnp.float32)
    onehot = (expert_ids[:, :, None] == jnp.arange(experts, dtype=jnp.int32)[None, None, :]).astype(
        jnp.float32
    )
    chosen_part = jnp.sum(partial_logits[:, None, :] * onehot, axis=2)
    flat_ids = expert_ids.reshape(-1)
    id_hits = (flat_ids[:, None] == jnp.arange(experts, dtype=jnp.int32)[None, :]).astype(jnp.int32)
    places = jnp.sum((jnp.cumsum(id_hits, axis=0) - 1) * id_hits, axis=1)
    slot_index = flat_ids * capacity + places
    slot_ids = jnp.arange(experts * capacity, dtype=jnp.int32)
    pick_hit = slot_ids[:, None] == slot_index[None, :]
    token_hit = pick_hit.reshape(experts * capacity, tok_rows, pick_count).any(axis=2)
    rows_in = jnp.concatenate([tokens, cotangent], axis=1)
    packed = jnp.dot(
        token_hit.astype(jnp.bfloat16), rows_in, preferred_element_type=jnp.float32
    ).astype(jnp.bfloat16)
    both = lax.all_to_all(
        packed.reshape(experts, capacity, 2 * shard_width),
        "ctx",
        split_axis=0,
        concat_axis=0,
        tiled=True,
    )
    slot_count = both.shape[0] * both.shape[1]
    half = slot_count // 2
    swapped = lax.axis_index("head") % 2 == 1

    def local_order(rows):
        turned = jnp.concatenate([rows[half:], rows[:half]], axis=0)
        return jnp.where(swapped, turned, rows)

    both = local_order(both.reshape(slot_count, 2 * shard_width))
    x_rows = both[:, :shard_width]
    cot_rows = both[:, shard_width:]
    gate_w = w_gate[0]
    up_w = w_up[0]
    down_w = w_down[0]
    gate_part = contract_last(x_rows, gate_w).astype(jnp.bfloat16)
    up_part = contract_last(x_rows, up_w).astype(jnp.bfloat16)
    back_part = contract_last(cot_rows, down_w).astype(jnp.bfloat16)
    head_count = lax.axis_size("head")
    partner = [(i, i ^ 1) for i in range(head_count)]
    same_core = [list(range(c, head_count, 2)) for c in range(2)]
    parts = jnp.stack([gate_part, up_part, back_part])
    pair_sum = (
        parts[:, :half].astype(jnp.float32)
        + lax.ppermute(parts[:, half:], "head", partner).astype(jnp.float32)
    ).astype(jnp.bfloat16)
    pair_sum, chosen_part = lax.optimization_barrier((pair_sum, chosen_part))
    mine = lax.psum(pair_sum, "head", axis_index_groups=same_core)
    chosen = head_sum(chosen_part)
    prob_pairs = jnp.stack(
        [jax.nn.sigmoid(chosen[:, 0] - chosen[:, 1]), jax.nn.sigmoid(chosen[:, 1] - chosen[:, 0])],
        axis=1,
    )
    pair_prod = prob_pairs[:, 0] * prob_pairs[:, 1]
    q_hi = pair_prod.astype(jnp.bfloat16).astype(jnp.float32)
    q_lo = pair_prod - q_hi
    pick_values = jnp.stack(
        [
            prob_pairs.reshape(-1),
            jnp.repeat(q_hi, pick_count),
            jnp.repeat(q_lo, pick_count),
            expert_ids[:, ::-1].reshape(-1).astype(jnp.float32),
        ],
        axis=0,
    )
    slot_values = jnp.sum(
        jnp.where(pick_hit[None], pick_values[:, None, :], 0.0), axis=2
    ).astype(jnp.bfloat16)
    recv_p = lax.all_to_all(
        slot_values.reshape(4, experts, capacity).transpose(1, 0, 2),
        "ctx",
        split_axis=0,
        concat_axis=0,
        tiled=True,
    )
    row_values = local_order(
        recv_p.transpose(0, 2, 1).reshape(slot_count, 4)
    ).T.astype(jnp.float32)
    mine, row_values = lax.optimization_barrier((mine, row_values))
    sums = jnp.concatenate([mine, lax.ppermute(mine, "head", partner)], axis=1)
    gate_sum, up_sum, back_sum = sums[0], sums[1], sums[2]
    prob_rows = row_values[0]
    pair_rows = row_values[1] + row_values[2]
    other_rows = row_values[3].astype(jnp.int32)
    gate_pre = gate_sum.astype(jnp.float32)
    up_pre = up_sum.astype(jnp.float32)
    hidden = forward_act(gate_pre, up_pre)
    back_proj = back_sum.astype(jnp.float32)
    gate_grad, up_grad = backward_act(gate_pre, up_pre, back_proj, prob_rows)
    out_rows = jnp.dot(hidden, down_w, preferred_element_type=jnp.float32).astype(jnp.bfloat16)
    dx_rows = (
        jnp.dot(gate_grad, gate_w, preferred_element_type=jnp.float32)
        + jnp.dot(up_grad, up_w, preferred_element_type=jnp.float32)
    ).astype(jnp.bfloat16)
    hidden_kept = lax.optimization_barrier(hidden)
    scaled = (prob_rows[:, None] * hidden_kept.astype(jnp.float32)).astype(jnp.bfloat16)
    grad_down = contract_rows(scaled, cot_rows).astype(jnp.bfloat16)[None]
    grad_gate = contract_rows(gate_grad, x_rows).astype(jnp.bfloat16)[None]
    grad_up = contract_rows(up_grad, x_rows).astype(jnp.bfloat16)[None]
    score_rows = jnp.sum(hidden.astype(jnp.float32) * back_proj, axis=1)
    own = lax.axis_index("ctx")
    expert_ids_row = jnp.arange(experts, dtype=jnp.int32)[None, :]
    direction = (expert_ids_row == own).astype(jnp.float32) - (
        expert_ids_row == other_rows[:, None]
    ).astype(jnp.float32)
    router_weight = (pair_rows * score_rows)[:, None] * direction
    router_part = jnp.dot(
        x_rows.astype(jnp.float32).T, router_weight, precision=lax.Precision.HIGHEST
    )
    s_hi = score_rows.astype(jnp.bfloat16)
    s_lo = (score_rows - s_hi.astype(jnp.float32)).astype(jnp.bfloat16)
    extra = jnp.zeros((slot_count, 128), jnp.bfloat16).at[:, 0].set(s_hi).at[:, 1].set(s_lo)
    back_both = lax.all_to_all(
        local_order(jnp.concatenate([out_rows, dx_rows, extra], axis=1)).reshape(
            ctx_count, capacity, 2 * shard_width + 128
        ),
        "ctx",
        split_axis=0,
        concat_axis=0,
        tiled=True,
    )
    router_part, grad_gate, grad_up, grad_down = lax.optimization_barrier(
        (router_part, grad_gate, grad_up, grad_down)
    )
    grad_router = ctx_sum(router_part)
    both_pairs = lax.dot_general(
        pick_hit.astype(jnp.bfloat16),
        back_both.reshape(experts * capacity, 2 * shard_width + 128),
        (((0,), (0,)), ((), ())),
        preferred_element_type=jnp.float32,
    ).reshape(tok_rows, pick_count, 2 * shard_width + 128)
    out_pairs = both_pairs[:, :, :shard_width].astype(jnp.bfloat16)
    dx_pairs = both_pairs[:, :, shard_width : 2 * shard_width].astype(jnp.bfloat16)
    score_grad = both_pairs[:, :, 2 * shard_width] + both_pairs[:, :, 2 * shard_width + 1]
    mixed = jnp.sum(prob_pairs[:, :, None] * out_pairs.astype(jnp.float32), axis=1).astype(
        jnp.bfloat16
    )
    logit_lead = prob_pairs[:, 0] * prob_pairs[:, 1] * (score_grad[:, 0] - score_grad[:, 1])
    logit_grad = jnp.stack([logit_lead, -logit_lead], axis=1)
    dense_grad = jnp.sum(logit_grad[:, :, None] * onehot, axis=1)
    router_term = jnp.dot(
        dense_grad, w_router.astype(jnp.float32).T, precision=lax.Precision.HIGHEST
    )
    grad_tokens = (
        dx_pairs[:, 0].astype(jnp.float32) + dx_pairs[:, 1].astype(jnp.float32) + router_term
    ).astype(jnp.bfloat16)
    return (mixed, grad_tokens, grad_router, grad_gate, grad_up, grad_down)


def solution(mesh):
    placed = (
        P("ctx", "head"),
        P("ctx", "head"),
        P("ctx", None),
        P("head", None),
        P("ctx", None, "head"),
        P("ctx", None, "head"),
        P("ctx", None, "head"),
    )
    return jax.shard_map(
        local,
        mesh=mesh,
        in_specs=placed,
        out_specs=(
            P("ctx", "head"),
            P("ctx", "head"),
            P("head", None),
            P("ctx", None, "head"),
            P("ctx", None, "head"),
            P("ctx", None, "head"),
        ),
        check_vma=False,
    )
```

```python
import jax
import jax.numpy as jnp
from jax import lax
from jax.sharding import PartitionSpec as P


def contract_rows(left, right):
    return lax.dot_general(
        left, right, (((0,), (0,)), ((), ())), preferred_element_type=jnp.float32
    )


def contract_last(left, right):
    return lax.dot_general(
        left, right, (((1,), (1,)), ((), ())), preferred_element_type=jnp.float32
    )


def forward_act(gate_pre, up_pre):
    sigma = jax.nn.sigmoid(gate_pre)
    active = gate_pre * sigma
    return (active * up_pre).astype(jnp.bfloat16)


def backward_act(gate_pre, up_pre, back_proj, prob_rows):
    sigma = jax.nn.sigmoid(gate_pre)
    active = gate_pre * sigma
    hidden_grad = prob_rows[:, None] * back_proj
    gate_grad = (hidden_grad * up_pre * sigma * (1.0 + gate_pre * (1.0 - sigma))).astype(
        jnp.bfloat16
    )
    up_grad = (hidden_grad * active).astype(jnp.bfloat16)
    return (gate_grad, up_grad)


def head_sum(part):
    count = lax.axis_size("head")
    spread = jnp.broadcast_to(part[None], (count,) + part.shape)
    gathered = lax.all_to_all(spread, "head", split_axis=0, concat_axis=0, tiled=True)
    return jnp.sum(gathered, axis=0)


def ctx_sum(part):
    count = lax.axis_size("ctx")
    rows = part.shape[0]
    pieces = part.reshape(count, rows // count, part.shape[1])
    mine = jnp.sum(lax.all_to_all(pieces, "ctx", split_axis=0, concat_axis=0, tiled=True), axis=0)
    spread = jnp.broadcast_to(mine[None], pieces.shape)
    return lax.all_to_all(spread, "ctx", split_axis=0, concat_axis=0, tiled=True).reshape(part.shape)


def local(tokens, cotangent, expert_ids, w_router, w_gate, w_up, w_down):
    ctx_count = lax.axis_size("ctx")
    tok_rows = tokens.shape[0]
    shard_width = tokens.shape[1]
    pick_count = expert_ids.shape[1]
    experts = w_router.shape[1]
    capacity = 3 * tok_rows * pick_count // (2 * experts)
    partial_logits = jnp.dot(tokens, w_router, preferred_element_type=jnp.float32)
    onehot = (expert_ids[:, :, None] == jnp.arange(experts, dtype=jnp.int32)[None, None, :]).astype(
        jnp.float32
    )
    chosen_part = jnp.sum(partial_logits[:, None, :] * onehot, axis=2)
    flat_ids = expert_ids.reshape(-1)
    id_hits = (flat_ids[:, None] == jnp.arange(experts, dtype=jnp.int32)[None, :]).astype(jnp.int32)
    places = jnp.sum((jnp.cumsum(id_hits, axis=0) - 1) * id_hits, axis=1)
    slot_index = flat_ids * capacity + places
    slot_ids = jnp.arange(experts * capacity, dtype=jnp.int32)
    pick_hit = slot_ids[:, None] == slot_index[None, :]
    token_hit = pick_hit.reshape(experts * capacity, tok_rows, pick_count).any(axis=2)
    rows_in = jnp.concatenate([tokens, cotangent], axis=1)
    packed = jnp.dot(
        token_hit.astype(jnp.bfloat16), rows_in, preferred_element_type=jnp.float32
    ).astype(jnp.bfloat16)
    both = lax.all_to_all(
        packed.reshape(experts, capacity, 2 * shard_width),
        "ctx",
        split_axis=0,
        concat_axis=0,
        tiled=True,
    )
    slot_count = both.shape[0] * both.shape[1]
    half = slot_count // 2
    swapped = lax.axis_index("head") % 2 == 1

    def local_order(rows):
        turned = jnp.concatenate([rows[half:], rows[:half]], axis=0)
        return jnp.where(swapped, turned, rows)

    both = local_order(both.reshape(slot_count, 2 * shard_width))
    x_rows = both[:, :shard_width]
    cot_rows = both[:, shard_width:]
    gate_w = w_gate[0]
    up_w = w_up[0]
    down_w = w_down[0]
    gate_part = contract_last(x_rows, gate_w).astype(jnp.bfloat16)
    up_part = contract_last(x_rows, up_w).astype(jnp.bfloat16)
    back_part = contract_last(cot_rows, down_w).astype(jnp.bfloat16)
    head_count = lax.axis_size("head")
    partner = [(i, i ^ 1) for i in range(head_count)]
    same_core = [list(range(c, head_count, 2)) for c in range(2)]
    parts = jnp.stack([gate_part, up_part, back_part])
    pair_sum = (
        parts[:, :half].astype(jnp.float32)
        + lax.ppermute(parts[:, half:], "head", partner).astype(jnp.float32)
    ).astype(jnp.bfloat16)
    pair_sum, chosen_part = lax.optimization_barrier((pair_sum, chosen_part))
    mine = lax.psum(pair_sum, "head", axis_index_groups=same_core)
    chosen = head_sum(chosen_part)
    prob_pairs = jnp.stack(
        [jax.nn.sigmoid(chosen[:, 0] - chosen[:, 1]), jax.nn.sigmoid(chosen[:, 1] - chosen[:, 0])],
        axis=1,
    )
    pair_prod = prob_pairs[:, 0] * prob_pairs[:, 1]
    q_hi = pair_prod.astype(jnp.bfloat16).astype(jnp.float32)
    q_lo = pair_prod - q_hi
    pick_values = jnp.stack(
        [
            prob_pairs.reshape(-1),
            jnp.repeat(q_hi, pick_count),
            jnp.repeat(q_lo, pick_count),
            expert_ids[:, ::-1].reshape(-1).astype(jnp.float32),
        ],
        axis=0,
    )
    slot_values = jnp.sum(
        jnp.where(pick_hit[None], pick_values[:, None, :], 0.0), axis=2
    ).astype(jnp.bfloat16)
    recv_p = lax.all_to_all(
        slot_values.reshape(4, experts, capacity).transpose(1, 0, 2),
        "ctx",
        split_axis=0,
        concat_axis=0,
        tiled=True,
    )
    row_values = local_order(
        recv_p.transpose(0, 2, 1).reshape(slot_count, 4)
    ).T.astype(jnp.float32)
    mine, row_values = lax.optimization_barrier((mine, row_values))
    halves = (mine.astype(jnp.float32), lax.ppermute(mine, "head", partner).astype(jnp.float32))
    prob_rows = row_values[0]
    pair_rows = row_values[1] + row_values[2]
    other_rows = row_values[3].astype(jnp.int32)
    prob_halves = (prob_rows[:half], prob_rows[half:])
    hidden = jnp.concatenate([forward_act(h[0], h[1]) for h in halves], axis=0)
    grads = [backward_act(h[0], h[1], h[2], p) for h, p in zip(halves, prob_halves)]
    gate_grad = jnp.concatenate([g[0] for g in grads], axis=0)
    up_grad = jnp.concatenate([g[1] for g in grads], axis=0)
    back_proj = jnp.concatenate([h[2] for h in halves], axis=0)
    out_rows = jnp.dot(hidden, down_w, preferred_element_type=jnp.float32).astype(jnp.bfloat16)
    dx_rows = (
        jnp.dot(gate_grad, gate_w, preferred_element_type=jnp.float32)
        + jnp.dot(up_grad, up_w, preferred_element_type=jnp.float32)
    ).astype(jnp.bfloat16)
    hidden_kept = lax.optimization_barrier(hidden)
    scaled = (prob_rows[:, None] * hidden_kept.astype(jnp.float32)).astype(jnp.bfloat16)
    grad_down = contract_rows(scaled, cot_rows).astype(jnp.bfloat16)[None]
    grad_gate = contract_rows(gate_grad, x_rows).astype(jnp.bfloat16)[None]
    grad_up = contract_rows(up_grad, x_rows).astype(jnp.bfloat16)[None]
    score_rows = jnp.sum(hidden.astype(jnp.float32) * back_proj, axis=1)
    own = lax.axis_index("ctx")
    expert_ids_row = jnp.arange(experts, dtype=jnp.int32)[None, :]
    direction = (expert_ids_row == own).astype(jnp.float32) - (
        expert_ids_row == other_rows[:, None]
    ).astype(jnp.float32)
    router_weight = (pair_rows * score_rows)[:, None] * direction
    router_part = jnp.dot(
        x_rows.astype(jnp.float32).T, router_weight, precision=lax.Precision.HIGHEST
    )
    s_hi = score_rows.astype(jnp.bfloat16)
    s_lo = (score_rows - s_hi.astype(jnp.float32)).astype(jnp.bfloat16)
    extra = jnp.zeros((slot_count, 128), jnp.bfloat16).at[:, 0].set(s_hi).at[:, 1].set(s_lo)
    back_both = lax.all_to_all(
        local_order(jnp.concatenate([out_rows, dx_rows, extra], axis=1)).reshape(
            ctx_count, capacity, 2 * shard_width + 128
        ),
        "ctx",
        split_axis=0,
        concat_axis=0,
        tiled=True,
    )
    grad_router = ctx_sum(router_part)
    both_pairs = lax.dot_general(
        pick_hit.astype(jnp.bfloat16),
        back_both.reshape(experts * capacity, 2 * shard_width + 128),
        (((0,), (0,)), ((), ())),
        preferred_element_type=jnp.float32,
    ).reshape(tok_rows, pick_count, 2 * shard_width + 128)
    out_pairs = both_pairs[:, :, :shard_width].astype(jnp.bfloat16)
    dx_pairs = both_pairs[:, :, shard_width : 2 * shard_width].astype(jnp.bfloat16)
    score_grad = both_pairs[:, :, 2 * shard_width] + both_pairs[:, :, 2 * shard_width + 1]
    mixed = jnp.sum(prob_pairs[:, :, None] * out_pairs.astype(jnp.float32), axis=1).astype(
        jnp.bfloat16
    )
    logit_lead = prob_pairs[:, 0] * prob_pairs[:, 1] * (score_grad[:, 0] - score_grad[:, 1])
    logit_grad = jnp.stack([logit_lead, -logit_lead], axis=1)
    dense_grad = jnp.sum(logit_grad[:, :, None] * onehot, axis=1)
    router_term = jnp.dot(
        dense_grad, w_router.astype(jnp.float32).T, precision=lax.Precision.HIGHEST
    )
    grad_tokens = (
        dx_pairs[:, 0].astype(jnp.float32) + dx_pairs[:, 1].astype(jnp.float32) + router_term
    ).astype(jnp.bfloat16)
    return (mixed, grad_tokens, grad_router, grad_gate, grad_up, grad_down)


def solution(mesh):
    placed = (
        P("ctx", "head"),
        P("ctx", "head"),
        P("ctx", None),
        P("head", None),
        P("ctx", None, "head"),
        P("ctx", None, "head"),
        P("ctx", None, "head"),
    )
    return jax.shard_map(
        local,
        mesh=mesh,
        in_specs=placed,
        out_specs=(
            P("ctx", "head"),
            P("ctx", "head"),
            P("head", None),
            P("ctx", None, "head"),
            P("ctx", None, "head"),
            P("ctx", None, "head"),
        ),
        check_vma=False,
    )
```

```python
import jax
import jax.numpy as jnp
from jax import lax
from jax.sharding import PartitionSpec as P


def contract_rows(left, right):
    return lax.dot_general(
        left, right, (((0,), (0,)), ((), ())), preferred_element_type=jnp.float32
    )


def contract_last(left, right):
    return lax.dot_general(
        left, right, (((1,), (1,)), ((), ())), preferred_element_type=jnp.float32
    )


def forward_act(gate_pre, up_pre):
    sigma = jax.nn.sigmoid(gate_pre)
    active = gate_pre * sigma
    return (active * up_pre).astype(jnp.bfloat16)


def backward_act(gate_pre, up_pre, back_proj, prob_rows):
    sigma = jax.nn.sigmoid(gate_pre)
    active = gate_pre * sigma
    hidden_grad = prob_rows[:, None] * back_proj
    gate_grad = (hidden_grad * up_pre * sigma * (1.0 + gate_pre * (1.0 - sigma))).astype(
        jnp.bfloat16
    )
    up_grad = (hidden_grad * active).astype(jnp.bfloat16)
    return (gate_grad, up_grad)


def head_sum(part):
    count = lax.axis_size("head")
    spread = jnp.broadcast_to(part[None], (count,) + part.shape)
    gathered = lax.all_to_all(spread, "head", split_axis=0, concat_axis=0, tiled=True)
    return jnp.sum(gathered, axis=0)


def ctx_sum(part):
    count = lax.axis_size("ctx")
    rows = part.shape[0]
    pieces = part.reshape(count, rows // count, part.shape[1])
    mine = jnp.sum(lax.all_to_all(pieces, "ctx", split_axis=0, concat_axis=0, tiled=True), axis=0)
    spread = jnp.broadcast_to(mine[None], pieces.shape)
    return lax.all_to_all(spread, "ctx", split_axis=0, concat_axis=0, tiled=True).reshape(part.shape)


def local(tokens, cotangent, expert_ids, w_router, w_gate, w_up, w_down):
    ctx_count = lax.axis_size("ctx")
    tok_rows = tokens.shape[0]
    shard_width = tokens.shape[1]
    pick_count = expert_ids.shape[1]
    experts = w_router.shape[1]
    capacity = 3 * tok_rows * pick_count // (2 * experts)
    partial_logits = jnp.dot(tokens, w_router, preferred_element_type=jnp.float32)
    onehot = (expert_ids[:, :, None] == jnp.arange(experts, dtype=jnp.int32)[None, None, :]).astype(
        jnp.float32
    )
    chosen_part = jnp.sum(partial_logits[:, None, :] * onehot, axis=2)
    flat_ids = expert_ids.reshape(-1)
    id_hits = (flat_ids[:, None] == jnp.arange(experts, dtype=jnp.int32)[None, :]).astype(jnp.int32)
    places = jnp.sum((jnp.cumsum(id_hits, axis=0) - 1) * id_hits, axis=1)
    slot_index = flat_ids * capacity + places
    slot_ids = jnp.arange(experts * capacity, dtype=jnp.int32)
    pick_hit = slot_ids[:, None] == slot_index[None, :]
    token_hit = pick_hit.reshape(experts * capacity, tok_rows, pick_count).any(axis=2)
    rows_in = jnp.concatenate([tokens, cotangent], axis=1)
    packed = jnp.dot(
        token_hit.astype(jnp.bfloat16), rows_in, preferred_element_type=jnp.float32
    ).astype(jnp.bfloat16)
    both = lax.all_to_all(
        packed.reshape(experts, capacity, 2 * shard_width),
        "ctx",
        split_axis=0,
        concat_axis=0,
        tiled=True,
    )
    slot_count = both.shape[0] * both.shape[1]
    half = slot_count // 2
    swapped = lax.axis_index("head") % 2 == 1

    def local_order(rows):
        turned = jnp.concatenate([rows[half:], rows[:half]], axis=0)
        return jnp.where(swapped, turned, rows)

    both = local_order(both.reshape(slot_count, 2 * shard_width))
    x_rows = both[:, :shard_width]
    cot_rows = both[:, shard_width:]
    gate_w = w_gate[0]
    up_w = w_up[0]
    down_w = w_down[0]
    gate_part = contract_last(x_rows, gate_w).astype(jnp.bfloat16)
    up_part = contract_last(x_rows, up_w).astype(jnp.bfloat16)
    back_part = contract_last(cot_rows, down_w).astype(jnp.bfloat16)
    head_count = lax.axis_size("head")
    partner = [(i, i ^ 1) for i in range(head_count)]
    same_core = [list(range(c, head_count, 2)) for c in range(2)]
    parts = jnp.stack([gate_part, up_part, back_part])
    pair_sum = (
        parts[:, :half].astype(jnp.float32)
        + lax.ppermute(parts[:, half:], "head", partner).astype(jnp.float32)
    ).astype(jnp.bfloat16)
    pair_sum, chosen_part = lax.optimization_barrier((pair_sum, chosen_part))
    mine = lax.psum(pair_sum, "head", axis_index_groups=same_core)
    chosen = head_sum(chosen_part)
    prob_pairs = jnp.stack(
        [jax.nn.sigmoid(chosen[:, 0] - chosen[:, 1]), jax.nn.sigmoid(chosen[:, 1] - chosen[:, 0])],
        axis=1,
    )
    pair_prod = prob_pairs[:, 0] * prob_pairs[:, 1]
    q_hi = pair_prod.astype(jnp.bfloat16).astype(jnp.float32)
    q_lo = pair_prod - q_hi
    pick_values = jnp.stack(
        [
            prob_pairs.reshape(-1),
            jnp.repeat(q_hi, pick_count),
            jnp.repeat(q_lo, pick_count),
            expert_ids[:, ::-1].reshape(-1).astype(jnp.float32),
        ],
        axis=0,
    )
    slot_values = lax.dot_general(
        pick_values.astype(jnp.bfloat16),
        pick_hit.astype(jnp.bfloat16),
        (((1,), (1,)), ((), ())),
        preferred_element_type=jnp.float32,
    ).astype(jnp.bfloat16)
    recv_p = lax.all_to_all(
        slot_values.reshape(4, experts, capacity).transpose(1, 0, 2),
        "ctx",
        split_axis=0,
        concat_axis=0,
        tiled=True,
    )
    row_values = local_order(
        recv_p.transpose(0, 2, 1).reshape(slot_count, 4)
    ).T.astype(jnp.float32)
    mine, row_values = lax.optimization_barrier((mine, row_values))
    halves = (mine.astype(jnp.float32), lax.ppermute(mine, "head", partner).astype(jnp.float32))
    prob_rows = row_values[0]
    pair_rows = row_values[1] + row_values[2]
    other_rows = row_values[3].astype(jnp.int32)
    prob_halves = (prob_rows[:half], prob_rows[half:])
    hidden = jnp.concatenate([forward_act(h[0], h[1]) for h in halves], axis=0)
    grads = [backward_act(h[0], h[1], h[2], p) for h, p in zip(halves, prob_halves)]
    gate_grad = jnp.concatenate([g[0] for g in grads], axis=0)
    up_grad = jnp.concatenate([g[1] for g in grads], axis=0)
    back_proj = jnp.concatenate([h[2] for h in halves], axis=0)
    out_rows = jnp.dot(hidden, down_w, preferred_element_type=jnp.float32).astype(jnp.bfloat16)
    dx_rows = (
        jnp.dot(gate_grad, gate_w, preferred_element_type=jnp.float32)
        + jnp.dot(up_grad, up_w, preferred_element_type=jnp.float32)
    ).astype(jnp.bfloat16)
    hidden_kept = lax.optimization_barrier(hidden)
    scaled = (prob_rows[:, None] * hidden_kept.astype(jnp.float32)).astype(jnp.bfloat16)
    grad_down = contract_rows(scaled, cot_rows).astype(jnp.bfloat16)[None]
    grad_gate = contract_rows(gate_grad, x_rows).astype(jnp.bfloat16)[None]
    grad_up = contract_rows(up_grad, x_rows).astype(jnp.bfloat16)[None]
    score_rows = jnp.sum(hidden.astype(jnp.float32) * back_proj, axis=1)
    own = lax.axis_index("ctx")
    expert_ids_row = jnp.arange(experts, dtype=jnp.int32)[None, :]
    direction = (expert_ids_row == own).astype(jnp.float32) - (
        expert_ids_row == other_rows[:, None]
    ).astype(jnp.float32)
    router_weight = (pair_rows * score_rows)[:, None] * direction
    router_part = jnp.dot(
        x_rows.astype(jnp.float32).T, router_weight, precision=lax.Precision.HIGHEST
    )
    s_hi = score_rows.astype(jnp.bfloat16)
    s_lo = (score_rows - s_hi.astype(jnp.float32)).astype(jnp.bfloat16)
    extra = jnp.zeros((slot_count, 128), jnp.bfloat16).at[:, 0].set(s_hi).at[:, 1].set(s_lo)
    back_both = lax.all_to_all(
        local_order(jnp.concatenate([out_rows, dx_rows, extra], axis=1)).reshape(
            ctx_count, capacity, 2 * shard_width + 128
        ),
        "ctx",
        split_axis=0,
        concat_axis=0,
        tiled=True,
    )
    grad_router = ctx_sum(router_part)
    both_pairs = lax.dot_general(
        pick_hit.astype(jnp.bfloat16),
        back_both.reshape(experts * capacity, 2 * shard_width + 128),
        (((0,), (0,)), ((), ())),
        preferred_element_type=jnp.float32,
    ).reshape(tok_rows, pick_count, 2 * shard_width + 128)
    out_pairs = both_pairs[:, :, :shard_width].astype(jnp.bfloat16)
    dx_pairs = both_pairs[:, :, shard_width : 2 * shard_width].astype(jnp.bfloat16)
    score_grad = both_pairs[:, :, 2 * shard_width] + both_pairs[:, :, 2 * shard_width + 1]
    mixed = jnp.sum(prob_pairs[:, :, None] * out_pairs.astype(jnp.float32), axis=1).astype(
        jnp.bfloat16
    )
    logit_lead = prob_pairs[:, 0] * prob_pairs[:, 1] * (score_grad[:, 0] - score_grad[:, 1])
    logit_grad = jnp.stack([logit_lead, -logit_lead], axis=1)
    dense_grad = jnp.sum(logit_grad[:, :, None] * onehot, axis=1)
    router_term = jnp.dot(
        dense_grad, w_router.astype(jnp.float32).T, precision=lax.Precision.HIGHEST
    )
    grad_tokens = (
        dx_pairs[:, 0].astype(jnp.float32) + dx_pairs[:, 1].astype(jnp.float32) + router_term
    ).astype(jnp.bfloat16)
    return (mixed, grad_tokens, grad_router, grad_gate, grad_up, grad_down)


def solution(mesh):
    placed = (
        P("ctx", "head"),
        P("ctx", "head"),
        P("ctx", None),
        P("head", None),
        P("ctx", None, "head"),
        P("ctx", None, "head"),
        P("ctx", None, "head"),
    )
    return jax.shard_map(
        local,
        mesh=mesh,
        in_specs=placed,
        out_specs=(
            P("ctx", "head"),
            P("ctx", "head"),
            P("head", None),
            P("ctx", None, "head"),
            P("ctx", None, "head"),
            P("ctx", None, "head"),
        ),
        check_vma=False,
    )
```

```python
import jax
import jax.numpy as jnp
from jax import lax
from jax.sharding import PartitionSpec as P


def contract_rows(left, right):
    return lax.dot_general(
        left, right, (((0,), (0,)), ((), ())), preferred_element_type=jnp.float32
    )


def contract_last(left, right):
    return lax.dot_general(
        left, right, (((1,), (1,)), ((), ())), preferred_element_type=jnp.float32
    )


def forward_act(gate_pre, up_pre):
    sigma = jax.nn.sigmoid(gate_pre)
    active = gate_pre * sigma
    return (active * up_pre).astype(jnp.bfloat16)


def backward_act(gate_pre, up_pre, back_proj, prob_rows):
    sigma = jax.nn.sigmoid(gate_pre)
    active = gate_pre * sigma
    hidden_grad = prob_rows[:, None] * back_proj
    gate_grad = (hidden_grad * up_pre * sigma * (1.0 + gate_pre * (1.0 - sigma))).astype(
        jnp.bfloat16
    )
    up_grad = (hidden_grad * active).astype(jnp.bfloat16)
    return (gate_grad, up_grad)


def head_sum(part):
    count = lax.axis_size("head")
    spread = jnp.broadcast_to(part[None], (count,) + part.shape)
    gathered = lax.all_to_all(spread, "head", split_axis=0, concat_axis=0, tiled=True)
    return jnp.sum(gathered, axis=0)


def ctx_sum(part):
    count = lax.axis_size("ctx")
    rows = part.shape[0]
    pieces = part.reshape(count, rows // count, part.shape[1])
    mine = jnp.sum(lax.all_to_all(pieces, "ctx", split_axis=0, concat_axis=0, tiled=True), axis=0)
    spread = jnp.broadcast_to(mine[None], pieces.shape)
    return lax.all_to_all(spread, "ctx", split_axis=0, concat_axis=0, tiled=True).reshape(part.shape)


def local(tokens, cotangent, expert_ids, w_router, w_gate, w_up, w_down):
    ctx_count = lax.axis_size("ctx")
    tok_rows = tokens.shape[0]
    shard_width = tokens.shape[1]
    pick_count = expert_ids.shape[1]
    experts = w_router.shape[1]
    capacity = 3 * tok_rows * pick_count // (2 * experts)
    partial_logits = jnp.dot(tokens, w_router, preferred_element_type=jnp.float32)
    onehot = (expert_ids[:, :, None] == jnp.arange(experts, dtype=jnp.int32)[None, None, :]).astype(
        jnp.float32
    )
    chosen_part = jnp.sum(partial_logits[:, None, :] * onehot, axis=2)
    flat_ids = expert_ids.reshape(-1)
    id_hits = (flat_ids[:, None] == jnp.arange(experts, dtype=jnp.int32)[None, :]).astype(jnp.int32)
    places = jnp.sum((jnp.cumsum(id_hits, axis=0) - 1) * id_hits, axis=1)
    slot_index = flat_ids * capacity + places
    slot_ids = jnp.arange(experts * capacity, dtype=jnp.int32)
    pick_hit = slot_ids[:, None] == slot_index[None, :]
    token_hit = pick_hit.reshape(experts * capacity, tok_rows, pick_count).any(axis=2)
    rows_in = jnp.concatenate([tokens, cotangent], axis=1)
    packed = jnp.dot(
        token_hit.astype(jnp.bfloat16), rows_in, preferred_element_type=jnp.float32
    ).astype(jnp.bfloat16)
    both = lax.all_to_all(
        packed.reshape(experts, capacity, 2 * shard_width),
        "ctx",
        split_axis=0,
        concat_axis=0,
        tiled=True,
    )
    slot_count = both.shape[0] * both.shape[1]
    half = slot_count // 2
    swapped = lax.axis_index("head") % 2 == 1

    def local_order(rows):
        turned = jnp.concatenate([rows[half:], rows[:half]], axis=0)
        return jnp.where(swapped, turned, rows)

    both = local_order(both.reshape(slot_count, 2 * shard_width))
    x_rows = both[:, :shard_width]
    cot_rows = both[:, shard_width:]
    gate_w = w_gate[0]
    up_w = w_up[0]
    down_w = w_down[0]
    gate_part = contract_last(x_rows, gate_w).astype(jnp.bfloat16)
    up_part = contract_last(x_rows, up_w).astype(jnp.bfloat16)
    back_part = contract_last(cot_rows, down_w).astype(jnp.bfloat16)
    head_count = lax.axis_size("head")
    partner = [(i, i ^ 1) for i in range(head_count)]
    same_core = [list(range(c, head_count, 2)) for c in range(2)]
    parts = jnp.stack([gate_part, up_part, back_part])
    pair_sum = (
        parts[:, :half].astype(jnp.float32)
        + lax.ppermute(parts[:, half:], "head", partner).astype(jnp.float32)
    ).astype(jnp.bfloat16)
    pair_sum, chosen_part = lax.optimization_barrier((pair_sum, chosen_part))
    mine = lax.psum(pair_sum, "head", axis_index_groups=same_core)
    chosen = head_sum(chosen_part)
    prob_pairs = jnp.stack(
        [jax.nn.sigmoid(chosen[:, 0] - chosen[:, 1]), jax.nn.sigmoid(chosen[:, 1] - chosen[:, 0])],
        axis=1,
    )
    pair_prod = prob_pairs[:, 0] * prob_pairs[:, 1]
    q_hi = pair_prod.astype(jnp.bfloat16).astype(jnp.float32)
    q_lo = pair_prod - q_hi
    pick_values = jnp.stack(
        [
            prob_pairs.reshape(-1),
            jnp.repeat(q_hi, pick_count),
            jnp.repeat(q_lo, pick_count),
            expert_ids[:, ::-1].reshape(-1).astype(jnp.float32),
        ],
        axis=0,
    )
    slot_values = jnp.sum(
        jnp.where(pick_hit[None], pick_values[:, None, :], 0.0), axis=2
    ).astype(jnp.bfloat16)
    recv_p = lax.all_to_all(
        slot_values.reshape(4, experts, capacity).transpose(1, 0, 2),
        "ctx",
        split_axis=0,
        concat_axis=0,
        tiled=True,
    )
    row_values = local_order(
        recv_p.transpose(0, 2, 1).reshape(slot_count, 4)
    ).T.astype(jnp.float32)
    mine, row_values = lax.optimization_barrier((mine, row_values))
    halves = (mine.astype(jnp.float32), lax.ppermute(mine, "head", partner).astype(jnp.float32))
    prob_rows = row_values[0]
    pair_rows = row_values[1] + row_values[2]
    other_rows = row_values[3].astype(jnp.int32)
    prob_halves = (prob_rows[:half], prob_rows[half:])
    hidden = jnp.concatenate([forward_act(h[0], h[1]) for h in halves], axis=0)
    grads = [backward_act(h[0], h[1], h[2], p) for h, p in zip(halves, prob_halves)]
    gate_grad = jnp.concatenate([g[0] for g in grads], axis=0)
    up_grad = jnp.concatenate([g[1] for g in grads], axis=0)
    back_proj = jnp.concatenate([h[2] for h in halves], axis=0)
    out_rows = jnp.dot(hidden, down_w, preferred_element_type=jnp.float32).astype(jnp.bfloat16)
    dx_rows = (
        jnp.dot(gate_grad, gate_w, preferred_element_type=jnp.float32)
        + jnp.dot(up_grad, up_w, preferred_element_type=jnp.float32)
    ).astype(jnp.bfloat16)
    scaled = (prob_rows[:, None] * hidden.astype(jnp.float32)).astype(jnp.bfloat16)
    grad_down = contract_rows(scaled, cot_rows).astype(jnp.bfloat16)[None]
    grad_gate = contract_rows(gate_grad, x_rows).astype(jnp.bfloat16)[None]
    grad_up = contract_rows(up_grad, x_rows).astype(jnp.bfloat16)[None]
    score_rows = jnp.sum(hidden.astype(jnp.float32) * back_proj, axis=1)
    own = lax.axis_index("ctx")
    expert_ids_row = jnp.arange(experts, dtype=jnp.int32)[None, :]
    direction = (expert_ids_row == own).astype(jnp.float32) - (
        expert_ids_row == other_rows[:, None]
    ).astype(jnp.float32)
    router_weight = (pair_rows * score_rows)[:, None] * direction
    router_part = jnp.dot(
        x_rows.astype(jnp.float32).T, router_weight, precision=lax.Precision.HIGHEST
    )
    s_hi = score_rows.astype(jnp.bfloat16)
    s_lo = (score_rows - s_hi.astype(jnp.float32)).astype(jnp.bfloat16)
    extra = jnp.zeros((slot_count, 128), jnp.bfloat16).at[:, 0].set(s_hi).at[:, 1].set(s_lo)
    back_both = lax.all_to_all(
        local_order(jnp.concatenate([out_rows, dx_rows, extra], axis=1)).reshape(
            ctx_count, capacity, 2 * shard_width + 128
        ),
        "ctx",
        split_axis=0,
        concat_axis=0,
        tiled=True,
    )
    grad_router = ctx_sum(router_part)
    both_pairs = lax.dot_general(
        pick_hit.astype(jnp.bfloat16),
        back_both.reshape(experts * capacity, 2 * shard_width + 128),
        (((0,), (0,)), ((), ())),
        preferred_element_type=jnp.float32,
    ).reshape(tok_rows, pick_count, 2 * shard_width + 128)
    out_pairs = both_pairs[:, :, :shard_width].astype(jnp.bfloat16)
    dx_pairs = both_pairs[:, :, shard_width : 2 * shard_width].astype(jnp.bfloat16)
    score_grad = both_pairs[:, :, 2 * shard_width] + both_pairs[:, :, 2 * shard_width + 1]
    mixed = jnp.sum(prob_pairs[:, :, None] * out_pairs.astype(jnp.float32), axis=1).astype(
        jnp.bfloat16
    )
    logit_lead = prob_pairs[:, 0] * prob_pairs[:, 1] * (score_grad[:, 0] - score_grad[:, 1])
    logit_grad = jnp.stack([logit_lead, -logit_lead], axis=1)
    dense_grad = jnp.sum(logit_grad[:, :, None] * onehot, axis=1)
    router_term = jnp.dot(
        dense_grad, w_router.astype(jnp.float32).T, precision=lax.Precision.HIGHEST
    )
    grad_tokens = (
        dx_pairs[:, 0].astype(jnp.float32) + dx_pairs[:, 1].astype(jnp.float32) + router_term
    ).astype(jnp.bfloat16)
    return (mixed, grad_tokens, grad_router, grad_gate, grad_up, grad_down)


def solution(mesh):
    placed = (
        P("ctx", "head"),
        P("ctx", "head"),
        P("ctx", None),
        P("head", None),
        P("ctx", None, "head"),
        P("ctx", None, "head"),
        P("ctx", None, "head"),
    )
    return jax.shard_map(
        local,
        mesh=mesh,
        in_specs=placed,
        out_specs=(
            P("ctx", "head"),
            P("ctx", "head"),
            P("head", None),
            P("ctx", None, "head"),
            P("ctx", None, "head"),
            P("ctx", None, "head"),
        ),
        check_vma=False,
    )
```
